256 devices in a mesh: tm: 128 (over z, y_lo, x, core), net: 2 (over y_hi).
Axes of the slice: x: 4, y: 4 (y_hi: 2, y_lo: 2; y = y_hi * 2 + y_lo), z: 8, core: 2. Of those that a mesh axis runs over, the one named last changes fastest.
Arguments:
- direction_nodal: float32 [1, 128, 2, 8192], P(None, 'tm', None, 'net'), may hold values from -27 to 27
- direction_capacity: float32 [1, 128, 65536], P(None, 'tm', 'net'), may hold values from -27 to 27
- residual_nodal: float32 [1, 128, 2, 8192], P(None, 'tm', None, 'net'), may hold values from -27 to 27
- residual_capacity: float32 [1, 128, 65536], P(None, 'tm', 'net'), may hold values from -27 to 27
- scale_flow: float32 [128, 12288], P('tm', 'net'), may hold values from 0.25 to 4
- scale_dispatch: float32 [128, 65536], P('tm', 'net'), may hold values from 0.25 to 4
- scale_storage: float32 [128, 2, 8192], P('tm', None, 'net'), may hold values from 0.25 to 4
- scale_capacity: float32 [65536], P('net'), may hold values from 0.02 to 0.3
- availability: float32 [128, 65536], P('tm', 'net'), may hold values from 0.05 to 1
- retention: float32 [8192], P('net'), may hold values from 0.5 to 1
- line_anchor: int32 [96], P('net'), may hold values from 0 to 63
- line_target: int32 [96], P('net'), may hold values from 0 to 63
- anchor_rows: int32 [12288], P('net'), may hold values from 0 to 127
- target_rows: int32 [12288], P('net'), may hold values from 0 to 127
- column_block: int32 [512], P('net'), may hold values from 0 to 63
- column_rows: int32 [65536], P('net'), may hold values from 0 to 127
Outputs:
- updated_nodal: float32 [1, 128, 2, 8192], P(None, 'tm', None, 'net')
- updated_capacity: float32 [1, 128, 65536], P(None, 'tm', 'net')
The draws below stay inside these ranges and needn't reach their ends.
All inputs are finite; a program needn't handle non-finite values.
Results may differ from the reference program's by a relative error of at most 0.00002.
Values sent between devices are 32-bit elements; how exact they have to be, the bound alone decides.
No kernel may reach another device: no remote copies, remote signals or barrier semaphores. Data moves between devices by JAX's collectives and lax.ppermute only.
A program may use at most 64 MiB of HBM per device.

```python
import math
import jax
import jax.numpy as jnp
from jax import lax

BUSES = 8192
LINES = 12288
COLUMNS = 65536
BLOCK = 128
SYSTEMS = 1
HOURS = 128


def scaled_field(key, shape):
    keys = jax.random.split(key, 3)
    hours = shape[1]
    position = jnp.arange(hours, dtype=jnp.float32) / float(max(hours - 1, 1))
    rising = jnp.exp(math.log(3.0) * position) * jnp.exp(jax.random.uniform(keys[0], (hours,), jnp.float32, 0.0, math.log(3.0)))
    hour_shape = [1] * len(shape)
    hour_shape[1] = hours
    rising = rising.reshape(hour_shape)
    column_scale = jnp.exp(jax.random.uniform(keys[1], (shape[-1],), jnp.float32, 0.0, math.log(3.0)))
    base = jnp.clip(jax.random.normal(keys[2], shape, jnp.float32), -4.0, 4.0)
    return (0.25 * base * rising * column_scale).astype(jnp.float32)


def draw_direction_nodal(key, part):
    return scaled_field(jax.random.fold_in(key, 11), (SYSTEMS, HOURS, 2, BUSES))


def draw_direction_capacity(key, part):
    return scaled_field(jax.random.fold_in(key, 12), (SYSTEMS, HOURS, COLUMNS))


def draw_residual_nodal(key, part):
    return scaled_field(jax.random.fold_in(key, 13), (SYSTEMS, HOURS, 2, BUSES))


def draw_residual_capacity(key, part):
    return scaled_field(jax.random.fold_in(key, 14), (SYSTEMS, HOURS, COLUMNS))


def plant(entries, stream_key, smallest, top_value):
    longest = entries.shape.index(max(entries.shape))
    spots = []
    for shift in (0, 1):
        where = [jax.random.randint(jax.random.fold_in(stream_key, axis), (), 0, length) for axis, length in enumerate(entries.shape)]
        where[longest] = (where[longest] + shift) % entries.shape[longest]
        spots.append(tuple(where))
    return entries.at[spots[0]].set(smallest).at[spots[1]].set(top_value)


def shard_levels(key, extent, cuts, low, largest):
    def one(axis_at, blocks):
        heights = jax.random.uniform(jax.random.fold_in(jax.random.fold_in(key, 6), axis_at), (blocks,), jnp.float32, low / len(cuts), largest / len(cuts))
        return jnp.repeat(jnp.exp(heights), extent[axis_at] // blocks).reshape((-1,) + (1,) * (len(extent) - axis_at - 1))

    factor_of = one(*cuts[0])
    for cut in cuts[1:]:
        factor_of = factor_of * one(*cut)
    return factor_of


def setup_inputs(seed: int = 0) -> dict:
    key_of = jax.random.split(jax.random.key(seed), 17)
    direction_nodal = draw_direction_nodal(jax.random.fold_in(key_of[16], 71), 0)
    direction_capacity = draw_direction_capacity(jax.random.fold_in(key_of[16], 71), 0)
    residual_nodal = draw_residual_nodal(jax.random.fold_in(key_of[16], 71), 0)
    residual_capacity = draw_residual_capacity(jax.random.fold_in(key_of[16], 71), 0)
    scale_flow = jnp.clip(jnp.exp(math.log(4.0) - 2.7725887 * jax.random.uniform(key_of[4], (HOURS, LINES), jnp.float32) ** shard_levels(key_of[4], (HOURS, LINES), ((0, 128), (1, 2)), -0.2, 0.2)), 0.25, 4.0)
    scale_dispatch = jnp.clip(jnp.exp(math.log(4.0) - 2.7725887 * jax.random.uniform(key_of[5], (HOURS, COLUMNS), jnp.float32) ** shard_levels(key_of[5], (HOURS, COLUMNS), ((0, 128), (1, 2)), -0.2, 0.2)), 0.25, 4.0)
    scale_storage = jnp.clip(jnp.exp(math.log(4.0) - 2.7725887 * jax.random.uniform(key_of[6], (HOURS, 2, BUSES), jnp.float32) ** shard_levels(key_of[6], (HOURS, 2, BUSES), ((0, 128), (2, 2)), -0.2, 0.2)), 0.25, 4.0)
    scale_capacity = jnp.clip(jnp.exp(math.log(0.3) - 2.7080503 * jax.random.uniform(key_of[7], (COLUMNS,), jnp.float32) ** shard_levels(key_of[7], (COLUMNS,), ((0, 2),), -0.2, 0.2)), 0.02, 0.3)
    availability = jnp.clip(0.05 + 0.95 * jax.random.uniform(key_of[8], (HOURS, COLUMNS), jnp.float32) ** shard_levels(key_of[8], (HOURS, COLUMNS), ((0, 128), (1, 2)), -0.2, 0.2), 0.05, 1.0)
    retention = jnp.clip(0.5 + 0.5 * jax.random.uniform(key_of[9], (BUSES,), jnp.float32) ** shard_levels(key_of[9], (BUSES,), ((0, 2),), -0.2, 0.2), 0.5, 1.0)
    line_anchor = plant(jax.random.randint(key_of[10], (LINES // BLOCK,), 0, BUSES // BLOCK), jax.random.fold_in(key_of[10], 1), 0, (BUSES // BLOCK) - 1).astype(jnp.int32)
    line_target = plant(jax.random.randint(key_of[11], (LINES // BLOCK,), 0, BUSES // BLOCK), jax.random.fold_in(key_of[11], 1), 0, (BUSES // BLOCK) - 1).astype(jnp.int32)
    anchor_rows = plant(jax.random.randint(key_of[12], (LINES,), 0, BLOCK), jax.random.fold_in(key_of[12], 1), 0, BLOCK - 1).astype(jnp.int32)
    target_rows = plant(jax.random.randint(key_of[13], (LINES,), 0, BLOCK), jax.random.fold_in(key_of[13], 1), 0, BLOCK - 1).astype(jnp.int32)
    column_block = plant(jax.random.randint(key_of[14], (COLUMNS // BLOCK,), 0, BUSES // BLOCK), jax.random.fold_in(key_of[14], 1), 0, (BUSES // BLOCK) - 1).astype(jnp.int32)
    column_rows = plant(jax.random.randint(key_of[15], (COLUMNS,), 0, BLOCK), jax.random.fold_in(key_of[15], 1), 0, BLOCK - 1).astype(jnp.int32)
    return {"direction_nodal": direction_nodal, "direction_capacity": direction_capacity, "residual_nodal": residual_nodal, "residual_capacity": residual_capacity, "scale_flow": scale_flow, "scale_dispatch": scale_dispatch, "scale_storage": scale_storage, "scale_capacity": scale_capacity, "availability": availability, "retention": retention, "line_anchor": line_anchor, "line_target": line_target, "anchor_rows": anchor_rows, "target_rows": target_rows, "column_block": column_block, "column_rows": column_rows}


DAMPING = 0.5


def reference(direction_nodal, direction_capacity, residual_nodal, residual_capacity, scale_flow, scale_dispatch, scale_storage, scale_capacity, availability, retention, line_anchor, line_target, anchor_rows, target_rows, column_block, column_rows):
    anchor = (jnp.repeat(line_anchor, BLOCK) * BLOCK + anchor_rows).astype(jnp.int32)
    target = (jnp.repeat(line_target, BLOCK) * BLOCK + target_rows).astype(jnp.int32)
    column_bus = (jnp.repeat(column_block, BLOCK) * BLOCK + column_rows).astype(jnp.int32)

    def one_system(pieces):
        search_nodal, search_capacity, left_nodal, left_capacity = pieces
        balance = search_nodal[:, 0, :]
        storage = search_nodal[:, 1, :]
        limit_dual = search_capacity
        flow_value = balance[:, anchor] - balance[:, target]
        dispatch_value = balance[:, column_bus] + limit_dual
        capacity_value = -jnp.sum(availability * limit_dual, axis=0)
        level_value = storage - retention * jnp.roll(storage, -1, axis=0)
        charge_value = balance - storage
        flow_scaled = scale_flow * flow_value
        dispatch_scaled = scale_dispatch * dispatch_value
        capacity_scaled = scale_capacity * capacity_value
        level_scaled = scale_storage[:, 0, :] * level_value
        charge_scaled = scale_storage[:, 1, :] * charge_value
        bus_terms = jnp.zeros_like(balance).at[:, anchor].add(flow_scaled)
        bus_terms = bus_terms.at[:, target].add(-flow_scaled).at[:, column_bus].add(dispatch_scaled)
        image_balance = bus_terms + charge_scaled + DAMPING * balance
        image_storage = level_scaled - retention * jnp.roll(level_scaled, 1, axis=0) - charge_scaled + DAMPING * storage
        image_limit = dispatch_scaled - availability * capacity_scaled[None, :] + DAMPING * limit_dual
        image_nodal = jnp.stack([image_balance, image_storage], axis=1)
        squares = jnp.sum(left_nodal * left_nodal) + jnp.sum(left_capacity * left_capacity)
        curvature = jnp.sum(search_nodal * image_nodal) + jnp.sum(search_capacity * image_limit)
        step_size = squares / curvature
        return (left_nodal - step_size * image_nodal, left_capacity - step_size * image_limit)

    updated_nodal, updated_capacity = lax.map(one_system, (direction_nodal, direction_capacity, residual_nodal, residual_capacity))
    return (updated_nodal, updated_capacity)
```

```python
import jax
import jax.numpy as jnp
from jax import lax
from jax.sharding import PartitionSpec as P

BLOCK = 128


DAMPING = 0.5


def passed_along(value, axis, steps):
    count = lax.axis_size(axis)
    pairs = [(source, (source + steps) % count) for source in range(count)]
    return lax.ppermute(value, axis, pairs)


def butterfly_sum(value, axis):
    count = lax.axis_size(axis)
    if count & (count - 1):
        return lax.psum(value, axis)
    step = 1
    while step < count:
        pairs = [(source, source ^ step) for source in range(count)]
        value = value + lax.ppermute(value, axis, pairs)
        step *= 2
    return value


def within_block_onehot(rows):
    picked = rows.reshape(-1, BLOCK)
    return picked[:, :, None] == jnp.arange(BLOCK, dtype=rows.dtype)[None, None, :]


def gather_blocks(table, blocks, onehot):
    lead = table.shape[:-1]
    tiled = table.reshape(lead + (-1, BLOCK))
    picked = jnp.take(tiled, blocks, axis=-2)
    values = jnp.sum(jnp.where(onehot, picked[..., :, None, :], 0.0), axis=-1)
    return values.reshape(lead + (-1,))


def scatter_blocks(values, blocks, onehot, count):
    lead = values.shape[:-1]
    tiled = values.reshape(lead + (-1, BLOCK))
    within = jnp.sum(jnp.where(onehot, tiled[..., :, :, None], 0.0), axis=-2)
    out = jnp.zeros(lead + (count, BLOCK), values.dtype)
    out = out.at[..., blocks, :].add(within)
    return out.reshape(lead + (-1,))


def body(
    direction_nodal,
    direction_capacity,
    residual_nodal,
    residual_capacity,
    scale_flow,
    scale_dispatch,
    scale_storage,
    scale_capacity,
    availability,
    retention,
    line_anchor,
    line_target,
    anchor_rows,
    target_rows,
    column_block,
    column_rows,
):
    net_count = lax.axis_size("net")
    net_index = lax.axis_index("net")
    lines = anchor_rows.shape[0]

    partial_sums = -jnp.sum(availability[None] * direction_capacity, axis=1)
    capacity_value = butterfly_sum(partial_sums, "tm")

    balance = direction_nodal[:, :, 0, :]
    storage = direction_nodal[:, :, 1, :]
    buses = balance.shape[-1] * net_count
    if net_count == 2:
        other = lax.ppermute(balance, "net", [(0, 1), (1, 0)])
        network = jnp.where(
            net_index == 0,
            jnp.concatenate([balance, other], axis=-1),
            jnp.concatenate([other, balance], axis=-1),
        )
    else:
        network = lax.all_gather(balance, "net", axis=2, tiled=True)

    blocks = jnp.concatenate([line_anchor, line_target, column_block])
    onehot = within_block_onehot(jnp.concatenate([anchor_rows, target_rows, column_rows]))
    gathered = gather_blocks(network, blocks, onehot)
    flow_value = gathered[..., :lines] - gathered[..., lines : 2 * lines]
    dispatch_value = gathered[..., 2 * lines :] + direction_capacity

    next_first = passed_along(storage[:, :1], "tm", -1)
    storage_next = jnp.concatenate([storage[:, 1:, :], next_first], axis=1)
    level_value = storage - retention * storage_next
    charge_value = balance - storage
    flow_scaled = scale_flow[None] * flow_value
    dispatch_scaled = scale_dispatch[None] * dispatch_value
    level_scaled = scale_storage[None, :, 0, :] * level_value
    charge_scaled = scale_storage[None, :, 1, :] * charge_value
    capacity_scaled = scale_capacity[None] * capacity_value
    squares_local = jnp.sum(residual_nodal * residual_nodal, axis=(1, 2, 3)) + jnp.sum(
        residual_capacity * residual_capacity, axis=(1, 2)
    )

    bus_terms = scatter_blocks(
        jnp.concatenate([flow_scaled, -flow_scaled, dispatch_scaled], axis=-1),
        blocks,
        onehot,
        buses // BLOCK,
    )
    if net_count == 2:
        half = buses // 2
        mine = lax.dynamic_slice_in_dim(bus_terms, net_index * half, half, axis=-1)
        theirs = lax.dynamic_slice_in_dim(bus_terms, (1 - net_index) * half, half, axis=-1)
        own_terms = mine + lax.ppermute(theirs, "net", [(0, 1), (1, 0)])
    else:
        own_terms = lax.psum_scatter(bus_terms, "net", scatter_dimension=2, tiled=True)
    image_balance = own_terms + charge_scaled + DAMPING * balance
    behind = passed_along(level_scaled[:, -1:], "tm", 1)
    level_before = jnp.concatenate([behind, level_scaled[:, :-1, :]], axis=1)
    image_storage = level_scaled - retention * level_before - charge_scaled + DAMPING * storage
    image_limit = (
        dispatch_scaled
        - availability[None] * capacity_scaled[:, None, :]
        + DAMPING * direction_capacity
    )
    image_nodal = jnp.stack([image_balance, image_storage], axis=2)
    curvature_local = jnp.sum(direction_nodal * image_nodal, axis=(1, 2, 3)) + jnp.sum(
        direction_capacity * image_limit, axis=(1, 2)
    )
    totals = butterfly_sum(jnp.stack([squares_local, curvature_local]), "tm")
    totals = butterfly_sum(totals, "net")
    step_size = totals[0] / totals[1]
    updated_nodal = residual_nodal - step_size[:, None, None, None] * image_nodal
    updated_capacity = residual_capacity - step_size[:, None, None] * image_limit
    return (updated_nodal, updated_capacity)


def solution(mesh):
    in_specs = (
        P(None, "tm", None, "net"),
        P(None, "tm", "net"),
        P(None, "tm", None, "net"),
        P(None, "tm", "net"),
        P("tm", "net"),
        P("tm", "net"),
        P("tm", None, "net"),
        P("net"),
        P("tm", "net"),
        P("net"),
        P("net"),
        P("net"),
        P("net"),
        P("net"),
        P("net"),
        P("net"),
    )
    out_specs = (P(None, "tm", None, "net"), P(None, "tm", "net"))
    return jax.shard_map(body, mesh=mesh, in_specs=in_specs, out_specs=out_specs, check_vma=False)
```

```python
import jax
import jax.numpy as jnp
from jax import lax
from jax.experimental import pallas as pl
from jax.sharding import PartitionSpec as P

BLOCK = 128


DAMPING = 0.5


def passed_along(value, axis, steps):
    count = lax.axis_size(axis)
    pairs = [(source, (source + steps) % count) for source in range(count)]
    return lax.ppermute(value, axis, pairs)


def butterfly_sum(value, axis):
    count = lax.axis_size(axis)
    if count & (count - 1):
        return lax.psum(value, axis)
    step = 1
    while step < count:
        pairs = [(source, source ^ step) for source in range(count)]
        value = value + lax.ppermute(value, axis, pairs)
        step *= 2
    return value


def pairwise_total(items):
    while len(items) > 1:
        items = [items[i] + items[i + 1] for i in range(0, len(items), 2)]
    return items[0]


def group_sum(value, axis, bits_per_step):
    count = lax.axis_size(axis)
    if count & (count - 1):
        return lax.psum(value, axis)
    total_bits = count.bit_length() - 1
    offset = 0
    while offset < total_bits:
        bits = min(bits_per_step, total_bits - offset)
        items = [value]
        for digit in range(1, 1 << bits):
            pairs = [(source, source ^ (digit << offset)) for source in range(count)]
            items.append(lax.ppermute(value, axis, pairs))
        value = pairwise_total(items)
        offset += bits
    return value


def lane_gather_kernel(table_ref, index_ref, out_ref):
    out_ref[...] = jnp.take_along_axis(
        table_ref[...], index_ref[...], axis=1, mode="promise_in_bounds"
    )


def lane_gather(table, index):
    return pl.pallas_call(
        lane_gather_kernel,
        out_shape=jax.ShapeDtypeStruct(table.shape, table.dtype),
    )(table, index)


def within_block_onehot(rows):
    picked = rows.reshape(-1, BLOCK)
    return picked[:, :, None] == jnp.arange(BLOCK, dtype=rows.dtype)[None, None, :]


def gather_blocks(table, blocks, rows):
    lead = table.shape[:-1]
    tiled = table.reshape(lead + (-1, BLOCK))
    picked = jnp.take(tiled, blocks, axis=-2)
    index = jnp.broadcast_to(rows.reshape(-1, BLOCK), picked.shape)
    values = lane_gather(picked.reshape(-1, BLOCK), index.reshape(-1, BLOCK))
    return values.reshape(lead + (-1,))


def scatter_blocks(values, blocks, onehot, count):
    lead = values.shape[:-1]
    tiled = values.reshape(lead + (-1, BLOCK))
    within = jnp.sum(jnp.where(onehot, tiled[..., :, :, None], 0.0), axis=-2)
    out = jnp.zeros(lead + (count, BLOCK), values.dtype)
    out = out.at[..., blocks, :].add(within)
    return out.reshape(lead + (-1,))


def body(
    direction_nodal,
    direction_capacity,
    residual_nodal,
    residual_capacity,
    scale_flow,
    scale_dispatch,
    scale_storage,
    scale_capacity,
    availability,
    retention,
    line_anchor,
    line_target,
    anchor_rows,
    target_rows,
    column_block,
    column_rows,
):
    net_count = lax.axis_size("net")
    net_index = lax.axis_index("net")
    lines = anchor_rows.shape[0]

    partial_sums = -jnp.sum(availability[None] * direction_capacity, axis=1)
    capacity_value = butterfly_sum(partial_sums, "tm")

    balance = direction_nodal[:, :, 0, :]
    storage = direction_nodal[:, :, 1, :]
    buses = balance.shape[-1] * net_count
    if net_count == 2:
        other = lax.ppermute(balance, "net", [(0, 1), (1, 0)])
        network = jnp.where(
            net_index == 0,
            jnp.concatenate([balance, other], axis=-1),
            jnp.concatenate([other, balance], axis=-1),
        )
    else:
        network = lax.all_gather(balance, "net", axis=2, tiled=True)

    blocks = jnp.concatenate([line_anchor, line_target, column_block])
    rows = jnp.concatenate([anchor_rows, target_rows, column_rows])
    onehot = within_block_onehot(rows)
    gathered = gather_blocks(network, blocks, rows)
    flow_value = gathered[..., :lines] - gathered[..., lines : 2 * lines]
    dispatch_value = gathered[..., 2 * lines :] + direction_capacity

    next_first = passed_along(storage[:, :1], "tm", -1)
    storage_next = jnp.concatenate([storage[:, 1:, :], next_first], axis=1)
    level_value = storage - retention * storage_next
    charge_value = balance - storage
    flow_scaled = scale_flow[None] * flow_value
    dispatch_scaled = scale_dispatch[None] * dispatch_value
    level_scaled = scale_storage[None, :, 0, :] * level_value
    charge_scaled = scale_storage[None, :, 1, :] * charge_value
    capacity_scaled = scale_capacity[None] * capacity_value
    squares_local = jnp.sum(residual_nodal * residual_nodal, axis=(1, 2, 3)) + jnp.sum(
        residual_capacity * residual_capacity, axis=(1, 2)
    )

    bus_terms = scatter_blocks(
        jnp.concatenate([flow_scaled, -flow_scaled, dispatch_scaled], axis=-1),
        blocks,
        onehot,
        buses // BLOCK,
    )
    if net_count == 2:
        half = buses // 2
        mine = lax.dynamic_slice_in_dim(bus_terms, net_index * half, half, axis=-1)
        theirs = lax.dynamic_slice_in_dim(bus_terms, (1 - net_index) * half, half, axis=-1)
        own_terms = mine + lax.ppermute(theirs, "net", [(0, 1), (1, 0)])
    else:
        own_terms = lax.psum_scatter(bus_terms, "net", scatter_dimension=2, tiled=True)
    image_balance = own_terms + charge_scaled + DAMPING * balance
    behind = passed_along(level_scaled[:, -1:], "tm", 1)
    level_before = jnp.concatenate([behind, level_scaled[:, :-1, :]], axis=1)
    image_storage = level_scaled - retention * level_before - charge_scaled + DAMPING * storage
    image_limit = (
        dispatch_scaled
        - availability[None] * capacity_scaled[:, None, :]
        + DAMPING * direction_capacity
    )
    image_nodal = jnp.stack([image_balance, image_storage], axis=2)
    curvature_local = jnp.sum(direction_nodal * image_nodal, axis=(1, 2, 3)) + jnp.sum(
        direction_capacity * (dispatch_scaled + DAMPING * direction_capacity), axis=(1, 2)
    )
    sums = group_sum(jnp.stack([squares_local, curvature_local]), "tm", 4)
    capacity_part = jnp.sum(capacity_scaled * capacity_value, axis=1)
    sums = sums + jnp.stack([jnp.zeros_like(capacity_part), capacity_part])
    totals = butterfly_sum(sums, "net")
    step_size = totals[0] / totals[1]
    updated_nodal = residual_nodal - step_size[:, None, None, None] * image_nodal
    updated_capacity = residual_capacity - step_size[:, None, None] * image_limit
    return (updated_nodal, updated_capacity)


def solution(mesh):
    in_specs = (
        P(None, "tm", None, "net"),
        P(None, "tm", "net"),
        P(None, "tm", None, "net"),
        P(None, "tm", "net"),
        P("tm", "net"),
        P("tm", "net"),
        P("tm", None, "net"),
        P("net"),
        P("tm", "net"),
        P("net"),
        P("net"),
        P("net"),
        P("net"),
        P("net"),
        P("net"),
        P("net"),
    )
    out_specs = (P(None, "tm", None, "net"), P(None, "tm", "net"))
    return jax.shard_map(body, mesh=mesh, in_specs=in_specs, out_specs=out_specs, check_vma=False)
```

```python
import jax
import jax.numpy as jnp
from jax import lax
from jax.experimental import pallas as pl
from jax.sharding import PartitionSpec as P

BLOCK = 128


DAMPING = 0.5


def passed_along(value, axis, steps):
    count = lax.axis_size(axis)
    pairs = [(source, (source + steps) % count) for source in range(count)]
    return lax.ppermute(value, axis, pairs)


def butterfly_sum(value, axis):
    count = lax.axis_size(axis)
    if count & (count - 1):
        return lax.psum(value, axis)
    step = 1
    while step < count:
        pairs = [(source, source ^ step) for source in range(count)]
        value = value + lax.ppermute(value, axis, pairs)
        step *= 2
    return value


def pairwise_total(items):
    while len(items) > 1:
        items = [items[i] + items[i + 1] for i in range(0, len(items), 2)]
    return items[0]


def group_sum(value, axis, bits_per_step):
    count = lax.axis_size(axis)
    if count & (count - 1):
        return lax.psum(value, axis)
    total_bits = count.bit_length() - 1
    offset = 0
    while offset < total_bits:
        bits = min(bits_per_step, total_bits - offset)
        items = [value]
        for digit in range(1, 1 << bits):
            pairs = [(source, source ^ (digit << offset)) for source in range(count)]
            items.append(lax.ppermute(value, axis, pairs))
        value = pairwise_total(items)
        offset += bits
    return value


def lane_gather_kernel(table_ref, index_ref, out_ref):
    out_ref[...] = jnp.take_along_axis(
        table_ref[...], index_ref[...], axis=1, mode="promise_in_bounds"
    )


def lane_gather(table, index):
    return pl.pallas_call(
        lane_gather_kernel,
        out_shape=jax.ShapeDtypeStruct(table.shape, table.dtype),
    )(table, index)


def lane_scatter_kernel(value_ref, index_ref, out_ref):
    tiles = BLOCK // 8
    for lane_tile in range(out_ref.shape[1] // BLOCK):
        lanes = pl.ds(lane_tile * BLOCK, BLOCK)

        def step(group, sums):
            start = pl.multiple_of(group * 8, 8)
            values = value_ref[pl.ds(start, 8), lanes]
            indices = index_ref[pl.ds(start, 8), lanes]
            for sub in range(8):
                value = jnp.broadcast_to(values[sub : sub + 1, :], (8, BLOCK))
                index = jnp.broadcast_to(indices[sub : sub + 1, :], (8, BLOCK))
                sums = tuple(
                    sums[tile]
                    + jnp.where(
                        index == lax.broadcasted_iota(jnp.int32, (8, BLOCK), 0) + 8 * tile,
                        value,
                        0.0,
                    )
                    for tile in range(tiles)
                )
            return sums

        zero = jnp.zeros((8, BLOCK), jnp.float32)
        sums = lax.fori_loop(0, tiles, step, (zero,) * tiles)
        for tile in range(tiles):
            out_ref[pl.ds(tile * 8, 8), lanes] = sums[tile]


def lane_scatter(values, index):
    count = values.shape[0]
    padded = -(-count // BLOCK) * BLOCK
    values_t = jnp.pad(values, ((0, padded - count), (0, 0))).T
    index_t = jnp.pad(index, ((0, padded - count), (0, 0))).T
    out = pl.pallas_call(
        lane_scatter_kernel,
        out_shape=jax.ShapeDtypeStruct((BLOCK, padded), values.dtype),
    )(values_t, index_t)
    return out.T[:count]


def gather_blocks(table, blocks, rows):
    lead = table.shape[:-1]
    tiled = table.reshape(lead + (-1, BLOCK))
    picked = jnp.take(tiled, blocks, axis=-2)
    index = jnp.broadcast_to(rows.reshape(-1, BLOCK), picked.shape)
    values = lane_gather(picked.reshape(-1, BLOCK), index.reshape(-1, BLOCK))
    return values.reshape(lead + (-1,))


def scatter_blocks(values, blocks, rows, count):
    lead = values.shape[:-1]
    tiled = values.reshape(lead + (-1, BLOCK))
    index = jnp.broadcast_to(rows.reshape(-1, BLOCK), tiled.shape)
    within = lane_scatter(tiled.reshape(-1, BLOCK), index.reshape(-1, BLOCK))
    within = within.reshape(tiled.shape)
    out = jnp.zeros(lead + (count, BLOCK), values.dtype)
    out = out.at[..., blocks, :].add(within)
    return out.reshape(lead + (-1,))


def body(
    direction_nodal,
    direction_capacity,
    residual_nodal,
    residual_capacity,
    scale_flow,
    scale_dispatch,
    scale_storage,
    scale_capacity,
    availability,
    retention,
    line_anchor,
    line_target,
    anchor_rows,
    target_rows,
    column_block,
    column_rows,
):
    net_count = lax.axis_size("net")
    net_index = lax.axis_index("net")
    lines = anchor_rows.shape[0]

    partial_sums = -jnp.sum(availability[None] * direction_capacity, axis=1)
    capacity_value = butterfly_sum(partial_sums, "tm")

    balance = direction_nodal[:, :, 0, :]
    storage = direction_nodal[:, :, 1, :]
    buses = balance.shape[-1] * net_count
    if net_count == 2:
        other = lax.ppermute(balance, "net", [(0, 1), (1, 0)])
        network = jnp.where(
            net_index == 0,
            jnp.concatenate([balance, other], axis=-1),
            jnp.concatenate([other, balance], axis=-1),
        )
    else:
        network = lax.all_gather(balance, "net", axis=2, tiled=True)

    blocks = jnp.concatenate([line_anchor, line_target, column_block])
    rows = jnp.concatenate([anchor_rows, target_rows, column_rows])
    gathered = gather_blocks(network, blocks, rows)
    flow_value = gathered[..., :lines] - gathered[..., lines : 2 * lines]
    dispatch_value = gathered[..., 2 * lines :] + direction_capacity

    next_first = passed_along(storage[:, :1], "tm", -1)
    storage_next = jnp.concatenate([storage[:, 1:, :], next_first], axis=1)
    level_value = storage - retention * storage_next
    charge_value = balance - storage
    flow_scaled = scale_flow[None] * flow_value
    dispatch_scaled = scale_dispatch[None] * dispatch_value
    level_scaled = scale_storage[None, :, 0, :] * level_value
    charge_scaled = scale_storage[None, :, 1, :] * charge_value
    capacity_scaled = scale_capacity[None] * capacity_value
    squares_local = jnp.sum(residual_nodal * residual_nodal, axis=(1, 2, 3)) + jnp.sum(
        residual_capacity * residual_capacity, axis=(1, 2)
    )

    bus_terms = scatter_blocks(
        jnp.concatenate([flow_scaled, -flow_scaled, dispatch_scaled], axis=-1),
        blocks,
        rows,
        buses // BLOCK,
    )
    if net_count == 2:
        half = buses // 2
        mine = lax.dynamic_slice_in_dim(bus_terms, net_index * half, half, axis=-1)
        theirs = lax.dynamic_slice_in_dim(bus_terms, (1 - net_index) * half, half, axis=-1)
        own_terms = mine + lax.ppermute(theirs, "net", [(0, 1), (1, 0)])
    else:
        own_terms = lax.psum_scatter(bus_terms, "net", scatter_dimension=2, tiled=True)
    image_balance = own_terms + charge_scaled + DAMPING * balance
    behind = passed_along(level_scaled[:, -1:], "tm", 1)
    level_before = jnp.concatenate([behind, level_scaled[:, :-1, :]], axis=1)
    image_storage = level_scaled - retention * level_before - charge_scaled + DAMPING * storage
    image_limit = (
        dispatch_scaled
        - availability[None] * capacity_scaled[:, None, :]
        + DAMPING * direction_capacity
    )
    image_nodal = jnp.stack([image_balance, image_storage], axis=2)
    curvature_local = jnp.sum(direction_nodal * image_nodal, axis=(1, 2, 3)) + jnp.sum(
        direction_capacity * (dispatch_scaled + DAMPING * direction_capacity), axis=(1, 2)
    )
    sums = butterfly_sum(jnp.stack([squares_local, curvature_local]), "tm")
    capacity_part = jnp.sum(capacity_scaled * capacity_value, axis=1)
    sums = sums + jnp.stack([jnp.zeros_like(capacity_part), capacity_part])
    totals = butterfly_sum(sums, "net")
    step_size = totals[0] / totals[1]
    updated_nodal = residual_nodal - step_size[:, None, None, None] * image_nodal
    updated_capacity = residual_capacity - step_size[:, None, None] * image_limit
    return (updated_nodal, updated_capacity)


def solution(mesh):
    in_specs = (
        P(None, "tm", None, "net"),
        P(None, "tm", "net"),
        P(None, "tm", None, "net"),
        P(None, "tm", "net"),
        P("tm", "net"),
        P("tm", "net"),
        P("tm", None, "net"),
        P("net"),
        P("tm", "net"),
        P("net"),
        P("net"),
        P("net"),
        P("net"),
        P("net"),
        P("net"),
        P("net"),
    )
    out_specs = (P(None, "tm", None, "net"), P(None, "tm", "net"))
    return jax.shard_map(body, mesh=mesh, in_specs=in_specs, out_specs=out_specs, check_vma=False)
```

```python
import jax
import jax.numpy as jnp
from jax import lax
from jax.experimental import pallas as pl
from jax.sharding import PartitionSpec as P

BLOCK = 128


DAMPING = 0.5


def passed_along(value, axis, steps):
    count = lax.axis_size(axis)
    pairs = [(source, (source + steps) % count) for source in range(count)]
    return lax.ppermute(value, axis, pairs)


def butterfly_sum(value, axis):
    count = lax.axis_size(axis)
    if count & (count - 1):
        return lax.psum(value, axis)
    step = 1
    while step < count:
        pairs = [(source, source ^ step) for source in range(count)]
        value = value + lax.ppermute(value, axis, pairs)
        step *= 2
    return value


def pairwise_total(items):
    while len(items) > 1:
        items = [items[i] + items[i + 1] for i in range(0, len(items), 2)]
    return items[0]


def group_sum(value, axis, bits_per_step):
    count = lax.axis_size(axis)
    if count & (count - 1):
        return lax.psum(value, axis)
    total_bits = count.bit_length() - 1
    offset = 0
    while offset < total_bits:
        bits = min(bits_per_step, total_bits - offset)
        items = [value]
        for digit in range(1, 1 << bits):
            pairs = [(source, source ^ (digit << offset)) for source in range(count)]
            items.append(lax.ppermute(value, axis, pairs))
        value = pairwise_total(items)
        offset += bits
    return value


def lane_gather_kernel(table_ref, index_ref, out_ref):
    out_ref[...] = jnp.take_along_axis(
        table_ref[...], index_ref[...], axis=1, mode="promise_in_bounds"
    )


def lane_gather(table, index):
    return pl.pallas_call(
        lane_gather_kernel,
        out_shape=jax.ShapeDtypeStruct(table.shape, table.dtype),
    )(table, index)


def lane_scatter_kernel(value_ref, index_ref, out_ref):
    tiles = BLOCK // 8
    for lane_tile in range(out_ref.shape[1] // BLOCK):
        lanes = pl.ds(lane_tile * BLOCK, BLOCK)

        def step(group, sums):
            start = pl.multiple_of(group * 8, 8)
            values = value_ref[pl.ds(start, 8), lanes]
            indices = index_ref[pl.ds(start, 8), lanes]
            for sub in range(8):
                value = jnp.broadcast_to(values[sub : sub + 1, :], (8, BLOCK))
                index = jnp.broadcast_to(indices[sub : sub + 1, :], (8, BLOCK))
                sums = tuple(
                    sums[tile]
                    + jnp.where(
                        index == lax.broadcasted_iota(jnp.int32, (8, BLOCK), 0) + 8 * tile,
                        value,
                        0.0,
                    )
                    for tile in range(tiles)
                )
            return sums

        zero = jnp.zeros((8, BLOCK), jnp.float32)
        sums = lax.fori_loop(0, tiles, step, (zero,) * tiles)
        for tile in range(tiles):
            out_ref[pl.ds(tile * 8, 8), lanes] = sums[tile]


def lane_scatter(values, index):
    count = values.shape[0]
    padded = -(-count // BLOCK) * BLOCK
    values_t = jnp.pad(values, ((0, padded - count), (0, 0))).T
    index_t = jnp.pad(index, ((0, padded - count), (0, 0))).T
    out = pl.pallas_call(
        lane_scatter_kernel,
        out_shape=jax.ShapeDtypeStruct((BLOCK, padded), values.dtype),
    )(values_t, index_t)
    return out.T[:count]


def gather_blocks(table, blocks, rows):
    lead = table.shape[:-1]
    tiled = table.reshape(lead + (-1, BLOCK))
    picked = jnp.take(tiled, blocks, axis=-2)
    index = jnp.broadcast_to(rows.reshape(-1, BLOCK), picked.shape)
    values = lane_gather(picked.reshape(-1, BLOCK), index.reshape(-1, BLOCK))
    return values.reshape(lead + (-1,))


def scatter_blocks(values, blocks, rows, count):
    lead = values.shape[:-1]
    tiled = values.reshape(lead + (-1, BLOCK))
    index = jnp.broadcast_to(rows.reshape(-1, BLOCK), tiled.shape)
    within = lane_scatter(tiled.reshape(-1, BLOCK), index.reshape(-1, BLOCK))
    within = within.reshape(tiled.shape)
    out = jnp.zeros(lead + (count, BLOCK), values.dtype)
    out = out.at[..., blocks, :].add(within)
    return out.reshape(lead + (-1,))


def body(
    direction_nodal,
    direction_capacity,
    residual_nodal,
    residual_capacity,
    scale_flow,
    scale_dispatch,
    scale_storage,
    scale_capacity,
    availability,
    retention,
    line_anchor,
    line_target,
    anchor_rows,
    target_rows,
    column_block,
    column_rows,
):
    net_count = lax.axis_size("net")
    net_index = lax.axis_index("net")
    lines = anchor_rows.shape[0]

    partial_sums = -jnp.sum(availability[None] * direction_capacity, axis=1)

    balance = direction_nodal[:, :, 0, :]
    storage = direction_nodal[:, :, 1, :]
    buses = balance.shape[-1] * net_count
    if net_count == 2:
        other = lax.ppermute(balance, "net", [(0, 1), (1, 0)])
        network = jnp.where(
            net_index == 0,
            jnp.concatenate([balance, other], axis=-1),
            jnp.concatenate([other, balance], axis=-1),
        )
    else:
        network = lax.all_gather(balance, "net", axis=2, tiled=True)

    blocks = jnp.concatenate([line_anchor, line_target, column_block])
    rows = jnp.concatenate([anchor_rows, target_rows, column_rows])
    gathered = gather_blocks(network, blocks, rows)
    flow_value = gathered[..., :lines] - gathered[..., lines : 2 * lines]
    dispatch_value = gathered[..., 2 * lines :] + direction_capacity

    next_first = passed_along(storage[:, :1], "tm", -1)
    storage_next = jnp.concatenate([storage[:, 1:, :], next_first], axis=1)
    level_value = storage - retention * storage_next
    charge_value = balance - storage
    flow_scaled = scale_flow[None] * flow_value
    dispatch_scaled = scale_dispatch[None] * dispatch_value
    level_scaled = scale_storage[None, :, 0, :] * level_value
    charge_scaled = scale_storage[None, :, 1, :] * charge_value
    squares_local = jnp.sum(residual_nodal * residual_nodal, axis=(1, 2, 3)) + jnp.sum(
        residual_capacity * residual_capacity, axis=(1, 2)
    )

    curvature_local = (
        jnp.sum(flow_scaled * flow_value, axis=(1, 2))
        + jnp.sum(dispatch_scaled * dispatch_value, axis=(1, 2))
        + jnp.sum(charge_scaled * charge_value, axis=(1, 2))
        + jnp.sum(level_scaled * level_value, axis=(1, 2))
        + DAMPING
        * (
            jnp.sum(direction_nodal * direction_nodal, axis=(1, 2, 3))
            + jnp.sum(direction_capacity * direction_capacity, axis=(1, 2))
        )
    )
    columns = partial_sums.shape[-1]
    scalars = jnp.stack([squares_local, curvature_local], axis=-1)
    packed = jnp.concatenate(
        [partial_sums, jnp.pad(scalars, ((0, 0), (0, BLOCK - 2)))], axis=-1
    )
    packed = butterfly_sum(packed, "tm")
    capacity_value = packed[:, :columns]
    capacity_scaled = scale_capacity[None] * capacity_value
    capacity_part = jnp.sum(capacity_scaled * capacity_value, axis=1)
    sums = packed[:, columns : columns + 2] + jnp.stack(
        [jnp.zeros_like(capacity_part), capacity_part], axis=-1
    )
    totals = butterfly_sum(sums, "net")

    bus_terms = scatter_blocks(
        jnp.concatenate([flow_scaled, -flow_scaled, dispatch_scaled], axis=-1),
        blocks,
        rows,
        buses // BLOCK,
    )
    if net_count == 2:
        half = buses // 2
        mine = lax.dynamic_slice_in_dim(bus_terms, net_index * half, half, axis=-1)
        theirs = lax.dynamic_slice_in_dim(bus_terms, (1 - net_index) * half, half, axis=-1)
        own_terms = mine + lax.ppermute(theirs, "net", [(0, 1), (1, 0)])
    else:
        own_terms = lax.psum_scatter(bus_terms, "net", scatter_dimension=2, tiled=True)
    image_balance = own_terms + charge_scaled + DAMPING * balance
    behind = passed_along(level_scaled[:, -1:], "tm", 1)
    level_before = jnp.concatenate([behind, level_scaled[:, :-1, :]], axis=1)
    image_storage = level_scaled - retention * level_before - charge_scaled + DAMPING * storage
    image_limit = (
        dispatch_scaled
        - availability[None] * capacity_scaled[:, None, :]
        + DAMPING * direction_capacity
    )
    image_nodal = jnp.stack([image_balance, image_storage], axis=2)
    step_size = totals[:, 0] / totals[:, 1]
    updated_nodal = residual_nodal - step_size[:, None, None, None] * image_nodal
    updated_capacity = residual_capacity - step_size[:, None, None] * image_limit
    return (updated_nodal, updated_capacity)


def solution(mesh):
    in_specs = (
        P(None, "tm", None, "net"),
        P(None, "tm", "net"),
        P(None, "tm", None, "net"),
        P(None, "tm", "net"),
        P("tm", "net"),
        P("tm", "net"),
        P("tm", None, "net"),
        P("net"),
        P("tm", "net"),
        P("net"),
        P("net"),
        P("net"),
        P("net"),
        P("net"),
        P("net"),
        P("net"),
    )
    out_specs = (P(None, "tm", None, "net"), P(None, "tm", "net"))
    return jax.shard_map(body, mesh=mesh, in_specs=in_specs, out_specs=out_specs, check_vma=False)
```

```python
import jax
import jax.numpy as jnp
from jax import lax
from jax.experimental import pallas as pl
from jax.sharding import PartitionSpec as P

BLOCK = 128


DAMPING = 0.5


def passed_along(value, axis, steps):
    count = lax.axis_size(axis)
    pairs = [(source, (source + steps) % count) for source in range(count)]
    return lax.ppermute(value, axis, pairs)


def butterfly_sum(value, axis, first=0, last=None):
    count = lax.axis_size(axis)
    bits = count.bit_length() - 1
    last = bits if last is None else min(last, bits)
    for bit in range(first, last):
        step = 1 << bit
        pairs = [(source, source ^ step) for source in range(count)]
        value = value + lax.ppermute(value, axis, pairs)
    return value


def is_power_of_two(count):
    return count & (count - 1) == 0


def pairwise_total(items):
    while len(items) > 1:
        items = [items[i] + items[i + 1] for i in range(0, len(items), 2)]
    return items[0]


def group_sum(value, axis, bits_per_step):
    count = lax.axis_size(axis)
    if count & (count - 1):
        return lax.psum(value, axis)
    total_bits = count.bit_length() - 1
    offset = 0
    while offset < total_bits:
        bits = min(bits_per_step, total_bits - offset)
        items = [value]
        for digit in range(1, 1 << bits):
            pairs = [(source, source ^ (digit << offset)) for source in range(count)]
            items.append(lax.ppermute(value, axis, pairs))
        value = pairwise_total(items)
        offset += bits
    return value


def lane_gather_kernel(table_ref, index_ref, out_ref):
    out_ref[...] = jnp.take_along_axis(
        table_ref[...], index_ref[...], axis=1, mode="promise_in_bounds"
    )


def lane_gather(table, index):
    return pl.pallas_call(
        lane_gather_kernel,
        out_shape=jax.ShapeDtypeStruct(table.shape, table.dtype),
    )(table, index)


def lane_scatter_kernel(value_ref, index_ref, out_ref):
    tiles = BLOCK // 8
    for lane_tile in range(out_ref.shape[1] // BLOCK):
        lanes = pl.ds(lane_tile * BLOCK, BLOCK)

        def step(group, sums):
            start = pl.multiple_of(group * 8, 8)
            values = value_ref[pl.ds(start, 8), lanes]
            indices = index_ref[pl.ds(start, 8), lanes]
            for sub in range(8):
                value = jnp.broadcast_to(values[sub : sub + 1, :], (8, BLOCK))
                index = jnp.broadcast_to(indices[sub : sub + 1, :], (8, BLOCK))
                sums = tuple(
                    sums[tile]
                    + jnp.where(
                        index == lax.broadcasted_iota(jnp.int32, (8, BLOCK), 0) + 8 * tile,
                        value,
                        0.0,
                    )
                    for tile in range(tiles)
                )
            return sums

        zero = jnp.zeros((8, BLOCK), jnp.float32)
        sums = lax.fori_loop(0, tiles, step, (zero,) * tiles)
        for tile in range(tiles):
            out_ref[pl.ds(tile * 8, 8), lanes] = sums[tile]


def lane_scatter(values, index):
    count = values.shape[0]
    padded = -(-count // BLOCK) * BLOCK
    values_t = jnp.pad(values, ((0, padded - count), (0, 0))).T
    index_t = jnp.pad(index, ((0, padded - count), (0, 0))).T
    out = pl.pallas_call(
        lane_scatter_kernel,
        out_shape=jax.ShapeDtypeStruct((BLOCK, padded), values.dtype),
    )(values_t, index_t)
    return out.T[:count]


def gather_blocks(table, blocks, rows):
    lead = table.shape[:-1]
    tiled = table.reshape(lead + (-1, BLOCK))
    picked = jnp.take(tiled, blocks, axis=-2)
    index = jnp.broadcast_to(rows.reshape(-1, BLOCK), picked.shape)
    values = lane_gather(picked.reshape(-1, BLOCK), index.reshape(-1, BLOCK))
    return values.reshape(lead + (-1,))


def scatter_blocks(values, blocks, rows, count):
    lead = values.shape[:-1]
    tiled = values.reshape(lead + (-1, BLOCK))
    index = jnp.broadcast_to(rows.reshape(-1, BLOCK), tiled.shape)
    within = lane_scatter(tiled.reshape(-1, BLOCK), index.reshape(-1, BLOCK))
    within = within.reshape(tiled.shape)
    out = jnp.zeros(lead + (count, BLOCK), values.dtype)
    out = out.at[..., blocks, :].add(within)
    return out.reshape(lead + (-1,))


def body(
    direction_nodal,
    direction_capacity,
    residual_nodal,
    residual_capacity,
    scale_flow,
    scale_dispatch,
    scale_storage,
    scale_capacity,
    availability,
    retention,
    line_anchor,
    line_target,
    anchor_rows,
    target_rows,
    column_block,
    column_rows,
):
    net_count = lax.axis_size("net")
    net_index = lax.axis_index("net")
    lines = anchor_rows.shape[0]

    tm_count = lax.axis_size("tm")
    partial_sums = -jnp.sum(availability[None] * direction_capacity, axis=1)

    balance = direction_nodal[:, :, 0, :]
    storage = direction_nodal[:, :, 1, :]
    buses = balance.shape[-1] * net_count
    next_first = passed_along(storage[:, :1], "tm", -1)
    if is_power_of_two(tm_count):
        early = butterfly_sum(partial_sums, "tm", 0, 4)
    else:
        early = lax.psum(partial_sums, "tm")
    if net_count == 2:
        other = lax.ppermute(balance, "net", [(0, 1), (1, 0)])
        early, other, next_first = lax.optimization_barrier((early, other, next_first))
        network = jnp.where(
            net_index == 0,
            jnp.concatenate([balance, other], axis=-1),
            jnp.concatenate([other, balance], axis=-1),
        )
    else:
        network = lax.all_gather(balance, "net", axis=2, tiled=True)
        early, network, next_first = lax.optimization_barrier((early, network, next_first))
    capacity_value = butterfly_sum(early, "tm", 4) if is_power_of_two(tm_count) else early

    blocks = jnp.concatenate([line_anchor, line_target, column_block])
    rows = jnp.concatenate([anchor_rows, target_rows, column_rows])
    gathered = gather_blocks(network, blocks, rows)
    flow_value = gathered[..., :lines] - gathered[..., lines : 2 * lines]
    dispatch_value = gathered[..., 2 * lines :] + direction_capacity

    storage_next = jnp.concatenate([storage[:, 1:, :], next_first], axis=1)
    level_value = storage - retention * storage_next
    charge_value = balance - storage
    flow_scaled = scale_flow[None] * flow_value
    dispatch_scaled = scale_dispatch[None] * dispatch_value
    level_scaled = scale_storage[None, :, 0, :] * level_value
    charge_scaled = scale_storage[None, :, 1, :] * charge_value
    squares_local = jnp.sum(residual_nodal * residual_nodal, axis=(1, 2, 3)) + jnp.sum(
        residual_capacity * residual_capacity, axis=(1, 2)
    )

    curvature_local = (
        jnp.sum(flow_scaled * flow_value, axis=(1, 2))
        + jnp.sum(dispatch_scaled * dispatch_value, axis=(1, 2))
        + jnp.sum(charge_scaled * charge_value, axis=(1, 2))
        + jnp.sum(level_scaled * level_value, axis=(1, 2))
        + DAMPING
        * (
            jnp.sum(direction_nodal * direction_nodal, axis=(1, 2, 3))
            + jnp.sum(direction_capacity * direction_capacity, axis=(1, 2))
        )
    )
    scalars = jnp.stack([squares_local, curvature_local], axis=-1)
    if is_power_of_two(tm_count):
        scalars = butterfly_sum(scalars, "tm")
    else:
        scalars = lax.psum(scalars, "tm")
    capacity_scaled = scale_capacity[None] * capacity_value
    capacity_part = jnp.sum(capacity_scaled * capacity_value, axis=1)
    sums = scalars + jnp.stack([jnp.zeros_like(capacity_part), capacity_part], axis=-1)
    totals = butterfly_sum(sums, "net") if is_power_of_two(net_count) else lax.psum(sums, "net")

    bus_terms = scatter_blocks(
        jnp.concatenate([flow_scaled, -flow_scaled, dispatch_scaled], axis=-1),
        blocks,
        rows,
        buses // BLOCK,
    )
    if net_count == 2:
        half = buses // 2
        mine = lax.dynamic_slice_in_dim(bus_terms, net_index * half, half, axis=-1)
        theirs = lax.dynamic_slice_in_dim(bus_terms, (1 - net_index) * half, half, axis=-1)
        own_terms = mine + lax.ppermute(theirs, "net", [(0, 1), (1, 0)])
    else:
        own_terms = lax.psum_scatter(bus_terms, "net", scatter_dimension=2, tiled=True)
    image_balance = own_terms + charge_scaled + DAMPING * balance
    behind = passed_along(level_scaled[:, -1:], "tm", 1)
    level_before = jnp.concatenate([behind, level_scaled[:, :-1, :]], axis=1)
    image_storage = level_scaled - retention * level_before - charge_scaled + DAMPING * storage
    image_limit = (
        dispatch_scaled
        - availability[None] * capacity_scaled[:, None, :]
        + DAMPING * direction_capacity
    )
    image_nodal = jnp.stack([image_balance, image_storage], axis=2)
    step_size = totals[:, 0] / totals[:, 1]
    updated_nodal = residual_nodal - step_size[:, None, None, None] * image_nodal
    updated_capacity = residual_capacity - step_size[:, None, None] * image_limit
    return (updated_nodal, updated_capacity)


def solution(mesh):
    in_specs = (
        P(None, "tm", None, "net"),
        P(None, "tm", "net"),
        P(None, "tm", None, "net"),
        P(None, "tm", "net"),
        P("tm", "net"),
        P("tm", "net"),
        P("tm", None, "net"),
        P("net"),
        P("tm", "net"),
        P("net"),
        P("net"),
        P("net"),
        P("net"),
        P("net"),
        P("net"),
        P("net"),
    )
    out_specs = (P(None, "tm", None, "net"), P(None, "tm", "net"))
    return jax.shard_map(body, mesh=mesh, in_specs=in_specs, out_specs=out_specs, check_vma=False)
```

```python
import jax
import jax.numpy as jnp
from jax import lax
from jax.experimental import pallas as pl
from jax.sharding import PartitionSpec as P

BLOCK = 128


DAMPING = 0.5


def passed_along(value, axis, steps):
    count = lax.axis_size(axis)
    pairs = [(source, (source + steps) % count) for source in range(count)]
    return lax.ppermute(value, axis, pairs)


def butterfly_sum(value, axis):
    count = lax.axis_size(axis)
    if count & (count - 1):
        return lax.psum(value, axis)
    step = 1
    while step < count:
        pairs = [(source, source ^ step) for source in range(count)]
        value = value + lax.ppermute(value, axis, pairs)
        step *= 2
    return value


def pairwise_total(items):
    while len(items) > 1:
        items = [items[i] + items[i + 1] for i in range(0, len(items), 2)]
    return items[0]


def group_sum(value, axis, bits_per_step):
    count = lax.axis_size(axis)
    if count & (count - 1):
        return lax.psum(value, axis)
    total_bits = count.bit_length() - 1
    offset = 0
    while offset < total_bits:
        bits = min(bits_per_step, total_bits - offset)
        items = [value]
        for digit in range(1, 1 << bits):
            pairs = [(source, source ^ (digit << offset)) for source in range(count)]
            items.append(lax.ppermute(value, axis, pairs))
        value = pairwise_total(items)
        offset += bits
    return value


def lane_gather_kernel(table_ref, index_ref, out_ref):
    out_ref[...] = jnp.take_along_axis(
        table_ref[...], index_ref[...], axis=1, mode="promise_in_bounds"
    )


def lane_gather(table, index):
    return pl.pallas_call(
        lane_gather_kernel,
        out_shape=jax.ShapeDtypeStruct(table.shape, table.dtype),
    )(table, index)


def lane_scatter_kernel(value_ref, index_ref, out_ref):
    tiles = BLOCK // 8
    for lane_tile in range(out_ref.shape[1] // BLOCK):
        lanes = pl.ds(lane_tile * BLOCK, BLOCK)

        def step(group, sums):
            start = pl.multiple_of(group * 8, 8)
            values = value_ref[pl.ds(start, 8), lanes]
            indices = index_ref[pl.ds(start, 8), lanes]
            for sub in range(8):
                value = jnp.broadcast_to(values[sub : sub + 1, :], (8, BLOCK))
                index = jnp.broadcast_to(indices[sub : sub + 1, :], (8, BLOCK))
                sums = tuple(
                    sums[tile]
                    + jnp.where(
                        index == lax.broadcasted_iota(jnp.int32, (8, BLOCK), 0) + 8 * tile,
                        value,
                        0.0,
                    )
                    for tile in range(tiles)
                )
            return sums

        zero = jnp.zeros((8, BLOCK), jnp.float32)
        sums = lax.fori_loop(0, tiles, step, (zero,) * tiles)
        for tile in range(tiles):
            out_ref[pl.ds(tile * 8, 8), lanes] = sums[tile]


def lane_scatter(values, index):
    count = values.shape[0]
    padded = -(-count // BLOCK) * BLOCK
    values_t = jnp.pad(values, ((0, padded - count), (0, 0))).T
    index_t = jnp.pad(index, ((0, padded - count), (0, 0))).T
    out = pl.pallas_call(
        lane_scatter_kernel,
        out_shape=jax.ShapeDtypeStruct((BLOCK, padded), values.dtype),
    )(values_t, index_t)
    return out.T[:count]


def gather_blocks(table, blocks, rows):
    lead = table.shape[:-1]
    tiled = table.reshape(lead + (-1, BLOCK))
    picked = jnp.take(tiled, blocks, axis=-2)
    index = jnp.broadcast_to(rows.reshape(-1, BLOCK), picked.shape)
    values = lane_gather(picked.reshape(-1, BLOCK), index.reshape(-1, BLOCK))
    return values.reshape(lead + (-1,))


def scatter_blocks(values, blocks, rows, count):
    lead = values.shape[:-1]
    tiled = values.reshape(lead + (-1, BLOCK))
    index = jnp.broadcast_to(rows.reshape(-1, BLOCK), tiled.shape)
    within = lane_scatter(tiled.reshape(-1, BLOCK), index.reshape(-1, BLOCK))
    within = within.reshape(tiled.shape)
    out = jnp.zeros(lead + (count, BLOCK), values.dtype)
    out = out.at[..., blocks, :].add(within)
    return out.reshape(lead + (-1,))


def body(
    direction_nodal,
    direction_capacity,
    residual_nodal,
    residual_capacity,
    scale_flow,
    scale_dispatch,
    scale_storage,
    scale_capacity,
    availability,
    retention,
    line_anchor,
    line_target,
    anchor_rows,
    target_rows,
    column_block,
    column_rows,
):
    net_count = lax.axis_size("net")
    net_index = lax.axis_index("net")
    lines = anchor_rows.shape[0]

    partial_sums = -jnp.sum(availability[None] * direction_capacity, axis=1)

    balance = direction_nodal[:, :, 0, :]
    storage = direction_nodal[:, :, 1, :]
    buses = balance.shape[-1] * net_count
    if net_count == 2:
        other = lax.ppermute(balance, "net", [(0, 1), (1, 0)])
        network = jnp.where(
            net_index == 0,
            jnp.concatenate([balance, other], axis=-1),
            jnp.concatenate([other, balance], axis=-1),
        )
    else:
        network = lax.all_gather(balance, "net", axis=2, tiled=True)

    blocks = jnp.concatenate([line_anchor, line_target, column_block])
    rows = jnp.concatenate([anchor_rows, target_rows, column_rows])
    gathered = gather_blocks(network, blocks, rows)
    flow_value = gathered[..., :lines] - gathered[..., lines : 2 * lines]
    dispatch_value = gathered[..., 2 * lines :] + direction_capacity

    first_hour, gathered = lax.optimization_barrier((storage[:, :1], gathered))
    next_first = passed_along(first_hour, "tm", -1)
    storage_next = jnp.concatenate([storage[:, 1:, :], next_first], axis=1)
    level_value = storage - retention * storage_next
    charge_value = balance - storage
    flow_scaled = scale_flow[None] * flow_value
    dispatch_scaled = scale_dispatch[None] * dispatch_value
    level_scaled = scale_storage[None, :, 0, :] * level_value
    charge_scaled = scale_storage[None, :, 1, :] * charge_value
    squares_local = jnp.sum(residual_nodal * residual_nodal, axis=(1, 2, 3)) + jnp.sum(
        residual_capacity * residual_capacity, axis=(1, 2)
    )

    curvature_local = (
        jnp.sum(flow_scaled * flow_value, axis=(1, 2))
        + jnp.sum(dispatch_scaled * dispatch_value, axis=(1, 2))
        + jnp.sum(charge_scaled * charge_value, axis=(1, 2))
        + jnp.sum(level_scaled * level_value, axis=(1, 2))
        + DAMPING
        * (
            jnp.sum(direction_nodal * direction_nodal, axis=(1, 2, 3))
            + jnp.sum(direction_capacity * direction_capacity, axis=(1, 2))
        )
    )
    columns = partial_sums.shape[-1]
    scalars = jnp.stack([squares_local, curvature_local], axis=-1)
    packed = jnp.concatenate(
        [partial_sums, jnp.pad(scalars, ((0, 0), (0, BLOCK - 2)))], axis=-1
    )
    packed = butterfly_sum(packed, "tm")
    capacity_value = packed[:, :columns]
    capacity_scaled = scale_capacity[None] * capacity_value
    capacity_part = jnp.sum(capacity_scaled * capacity_value, axis=1)
    sums = packed[:, columns : columns + 2] + jnp.stack(
        [jnp.zeros_like(capacity_part), capacity_part], axis=-1
    )
    image_limit = (
        dispatch_scaled
        - availability[None] * capacity_scaled[:, None, :]
        + DAMPING * direction_capacity
    )
    sums, image_limit = lax.optimization_barrier((sums, image_limit))
    totals = butterfly_sum(sums, "net")

    bus_terms = scatter_blocks(
        jnp.concatenate([flow_scaled, -flow_scaled, dispatch_scaled], axis=-1),
        blocks,
        rows,
        buses // BLOCK,
    )
    if net_count == 2:
        half = buses // 2
        mine = lax.dynamic_slice_in_dim(bus_terms, net_index * half, half, axis=-1)
        theirs = lax.dynamic_slice_in_dim(bus_terms, (1 - net_index) * half, half, axis=-1)
        own_terms = mine + lax.ppermute(theirs, "net", [(0, 1), (1, 0)])
    else:
        own_terms = lax.psum_scatter(bus_terms, "net", scatter_dimension=2, tiled=True)
    image_balance = own_terms + charge_scaled + DAMPING * balance
    behind = passed_along(level_scaled[:, -1:], "tm", 1)
    level_before = jnp.concatenate([behind, level_scaled[:, :-1, :]], axis=1)
    image_storage = level_scaled - retention * level_before - charge_scaled + DAMPING * storage
    image_nodal = jnp.stack([image_balance, image_storage], axis=2)
    step_size = totals[:, 0] / totals[:, 1]
    updated_nodal = residual_nodal - step_size[:, None, None, None] * image_nodal
    updated_capacity = residual_capacity - step_size[:, None, None] * image_limit
    return (updated_nodal, updated_capacity)


def solution(mesh):
    in_specs = (
        P(None, "tm", None, "net"),
        P(None, "tm", "net"),
        P(None, "tm", None, "net"),
        P(None, "tm", "net"),
        P("tm", "net"),
        P("tm", "net"),
        P("tm", None, "net"),
        P("net"),
        P("tm", "net"),
        P("net"),
        P("net"),
        P("net"),
        P("net"),
        P("net"),
        P("net"),
        P("net"),
    )
    out_specs = (P(None, "tm", None, "net"), P(None, "tm", "net"))
    return jax.shard_map(body, mesh=mesh, in_specs=in_specs, out_specs=out_specs, check_vma=False)
```

```python
import jax
import jax.numpy as jnp
from jax import lax
from jax.experimental import pallas as pl
from jax.sharding import PartitionSpec as P

BLOCK = 128


DAMPING = 0.5


def passed_along(value, axis, steps):
    count = lax.axis_size(axis)
    pairs = [(source, (source + steps) % count) for source in range(count)]
    return lax.ppermute(value, axis, pairs)


def from_next(value, axis):
    count = lax.axis_size(axis)
    if count % 2 or count < 4:
        return passed_along(value, axis, -1)
    pair = lax.ppermute(value, axis, [(source, source ^ 1) for source in range(count)])
    swap = lax.ppermute(
        value,
        axis,
        [(source, (source + 1) % count if source % 2 else (source - 1) % count) for source in range(count)],
    )
    return jnp.where(lax.axis_index(axis) % 2 == 0, pair, swap)


def butterfly_sum(value, axis):
    count = lax.axis_size(axis)
    if count & (count - 1):
        return lax.psum(value, axis)
    step = 1
    while step < count:
        pairs = [(source, source ^ step) for source in range(count)]
        value = value + lax.ppermute(value, axis, pairs)
        step *= 2
    return value


def pairwise_total(items):
    while len(items) > 1:
        items = [items[i] + items[i + 1] for i in range(0, len(items), 2)]
    return items[0]


def group_sum(value, axis, bits_per_step):
    count = lax.axis_size(axis)
    if count & (count - 1):
        return lax.psum(value, axis)
    total_bits = count.bit_length() - 1
    offset = 0
    while offset < total_bits:
        bits = min(bits_per_step, total_bits - offset)
        items = [value]
        for digit in range(1, 1 << bits):
            pairs = [(source, source ^ (digit << offset)) for source in range(count)]
            items.append(lax.ppermute(value, axis, pairs))
        value = pairwise_total(items)
        offset += bits
    return value


def lane_gather_kernel(table_ref, index_ref, out_ref):
    out_ref[...] = jnp.take_along_axis(
        table_ref[...], index_ref[...], axis=1, mode="promise_in_bounds"
    )


def lane_gather(table, index):
    return pl.pallas_call(
        lane_gather_kernel,
        out_shape=jax.ShapeDtypeStruct(table.shape, table.dtype),
    )(table, index)


def lane_scatter_kernel(value_ref, index_ref, out_ref):
    tiles = BLOCK // 8
    for lane_tile in range(out_ref.shape[1] // BLOCK):
        lanes = pl.ds(lane_tile * BLOCK, BLOCK)

        def step(group, sums):
            start = pl.multiple_of(group * 8, 8)
            values = value_ref[pl.ds(start, 8), lanes]
            indices = index_ref[pl.ds(start, 8), lanes]
            for sub in range(8):
                value = jnp.broadcast_to(values[sub : sub + 1, :], (8, BLOCK))
                index = jnp.broadcast_to(indices[sub : sub + 1, :], (8, BLOCK))
                sums = tuple(
                    sums[tile]
                    + jnp.where(
                        index == lax.broadcasted_iota(jnp.int32, (8, BLOCK), 0) + 8 * tile,
                        value,
                        0.0,
                    )
                    for tile in range(tiles)
                )
            return sums

        zero = jnp.zeros((8, BLOCK), jnp.float32)
        sums = lax.fori_loop(0, tiles, step, (zero,) * tiles)
        for tile in range(tiles):
            out_ref[pl.ds(tile * 8, 8), lanes] = sums[tile]


def lane_scatter(values, index):
    count = values.shape[0]
    padded = -(-count // BLOCK) * BLOCK
    values_t = jnp.pad(values, ((0, padded - count), (0, 0))).T
    index_t = jnp.pad(index, ((0, padded - count), (0, 0))).T
    out = pl.pallas_call(
        lane_scatter_kernel,
        out_shape=jax.ShapeDtypeStruct((BLOCK, padded), values.dtype),
    )(values_t, index_t)
    return out.T[:count]


def gather_blocks(table, blocks, rows):
    lead = table.shape[:-1]
    tiled = table.reshape(lead + (-1, BLOCK))
    picked = jnp.take(tiled, blocks, axis=-2)
    index = jnp.broadcast_to(rows.reshape(-1, BLOCK), picked.shape)
    values = lane_gather(picked.reshape(-1, BLOCK), index.reshape(-1, BLOCK))
    return values.reshape(lead + (-1,))


def scatter_blocks(values, blocks, rows, count):
    lead = values.shape[:-1]
    tiled = values.reshape(lead + (-1, BLOCK))
    index = jnp.broadcast_to(rows.reshape(-1, BLOCK), tiled.shape)
    within = lane_scatter(tiled.reshape(-1, BLOCK), index.reshape(-1, BLOCK))
    within = within.reshape(tiled.shape)
    out = jnp.zeros(lead + (count, BLOCK), values.dtype)
    out = out.at[..., blocks, :].add(within)
    return out.reshape(lead + (-1,))


def body(
    direction_nodal,
    direction_capacity,
    residual_nodal,
    residual_capacity,
    scale_flow,
    scale_dispatch,
    scale_storage,
    scale_capacity,
    availability,
    retention,
    line_anchor,
    line_target,
    anchor_rows,
    target_rows,
    column_block,
    column_rows,
):
    net_count = lax.axis_size("net")
    net_index = lax.axis_index("net")
    lines = anchor_rows.shape[0]

    partial_sums = -jnp.sum(availability[None] * direction_capacity, axis=1)

    balance = direction_nodal[:, :, 0, :]
    storage = direction_nodal[:, :, 1, :]
    buses = balance.shape[-1] * net_count
    if net_count == 2:
        other = lax.ppermute(balance, "net", [(0, 1), (1, 0)])
        network = jnp.where(
            net_index == 0,
            jnp.concatenate([balance, other], axis=-1),
            jnp.concatenate([other, balance], axis=-1),
        )
    else:
        network = lax.all_gather(balance, "net", axis=2, tiled=True)

    blocks = jnp.concatenate([line_anchor, line_target, column_block])
    rows = jnp.concatenate([anchor_rows, target_rows, column_rows])
    gathered = gather_blocks(network, blocks, rows)
    flow_value = gathered[..., :lines] - gathered[..., lines : 2 * lines]
    dispatch_value = gathered[..., 2 * lines :] + direction_capacity

    first_hour, gathered = lax.optimization_barrier((storage[:, :1], gathered))
    next_first = from_next(first_hour, "tm")
    storage_next = jnp.concatenate([storage[:, 1:, :], next_first], axis=1)
    level_value = storage - retention * storage_next
    charge_value = balance - storage
    flow_scaled = scale_flow[None] * flow_value
    dispatch_scaled = scale_dispatch[None] * dispatch_value
    level_scaled = scale_storage[None, :, 0, :] * level_value
    charge_scaled = scale_storage[None, :, 1, :] * charge_value
    squares_local = jnp.sum(residual_nodal * residual_nodal, axis=(1, 2, 3)) + jnp.sum(
        residual_capacity * residual_capacity, axis=(1, 2)
    )

    curvature_local = (
        jnp.sum(flow_scaled * flow_value, axis=(1, 2))
        + jnp.sum(dispatch_scaled * dispatch_value, axis=(1, 2))
        + jnp.sum(charge_scaled * charge_value, axis=(1, 2))
        + jnp.sum(level_scaled * level_value, axis=(1, 2))
        + DAMPING
        * (
            jnp.sum(direction_nodal * direction_nodal, axis=(1, 2, 3))
            + jnp.sum(direction_capacity * direction_capacity, axis=(1, 2))
        )
    )
    columns = partial_sums.shape[-1]
    scalars = jnp.stack([squares_local, curvature_local], axis=-1)
    packed = jnp.concatenate(
        [partial_sums, jnp.pad(scalars, ((0, 0), (0, BLOCK - 2)))], axis=-1
    )
    packed = butterfly_sum(packed, "tm")
    capacity_value = packed[:, :columns]
    capacity_scaled = scale_capacity[None] * capacity_value
    capacity_part = jnp.sum(capacity_scaled * capacity_value, axis=1)
    sums = packed[:, columns : columns + 2] + jnp.stack(
        [jnp.zeros_like(capacity_part), capacity_part], axis=-1
    )
    image_limit = (
        dispatch_scaled
        - availability[None] * capacity_scaled[:, None, :]
        + DAMPING * direction_capacity
    )
    sums, image_limit = lax.optimization_barrier((sums, image_limit))
    totals = butterfly_sum(sums, "net")

    bus_terms = scatter_blocks(
        jnp.concatenate([flow_scaled, -flow_scaled, dispatch_scaled], axis=-1),
        blocks,
        rows,
        buses // BLOCK,
    )
    if net_count == 2:
        half = buses // 2
        mine = lax.dynamic_slice_in_dim(bus_terms, net_index * half, half, axis=-1)
        theirs = lax.dynamic_slice_in_dim(bus_terms, (1 - net_index) * half, half, axis=-1)
        own_terms = mine + lax.ppermute(theirs, "net", [(0, 1), (1, 0)])
    else:
        own_terms = lax.psum_scatter(bus_terms, "net", scatter_dimension=2, tiled=True)
    image_balance = own_terms + charge_scaled + DAMPING * balance
    behind = passed_along(level_scaled[:, -1:], "tm", 1)
    level_before = jnp.concatenate([behind, level_scaled[:, :-1, :]], axis=1)
    image_storage = level_scaled - retention * level_before - charge_scaled + DAMPING * storage
    image_nodal = jnp.stack([image_balance, image_storage], axis=2)
    step_size = totals[:, 0] / totals[:, 1]
    updated_nodal = residual_nodal - step_size[:, None, None, None] * image_nodal
    updated_capacity = residual_capacity - step_size[:, None, None] * image_limit
    return (updated_nodal, updated_capacity)


def solution(mesh):
    in_specs = (
        P(None, "tm", None, "net"),
        P(None, "tm", "net"),
        P(None, "tm", None, "net"),
        P(None, "tm", "net"),
        P("tm", "net"),
        P("tm", "net"),
        P("tm", None, "net"),
        P("net"),
        P("tm", "net"),
        P("net"),
        P("net"),
        P("net"),
        P("net"),
        P("net"),
        P("net"),
        P("net"),
    )
    out_specs = (P(None, "tm", None, "net"), P(None, "tm", "net"))
    return jax.shard_map(body, mesh=mesh, in_specs=in_specs, out_specs=out_specs, check_vma=False)
```

```python
import jax
import jax.numpy as jnp
from jax import lax
from jax.experimental import pallas as pl
from jax.sharding import PartitionSpec as P

BLOCK = 128


DAMPING = 0.5


def passed_along(value, axis, steps):
    count = lax.axis_size(axis)
    pairs = [(source, (source + steps) % count) for source in range(count)]
    return lax.ppermute(value, axis, pairs)


def butterfly_sum(value, axis):
    count = lax.axis_size(axis)
    if count & (count - 1):
        return lax.psum(value, axis)
    step = 1
    while step < count:
        pairs = [(source, source ^ step) for source in range(count)]
        value = value + lax.ppermute(value, axis, pairs)
        step *= 2
    return value


def pairwise_total(items):
    while len(items) > 1:
        items = [items[i] + items[i + 1] for i in range(0, len(items), 2)]
    return items[0]


def group_sum(value, axis, bits_per_step):
    count = lax.axis_size(axis)
    if count & (count - 1):
        return lax.psum(value, axis)
    total_bits = count.bit_length() - 1
    offset = 0
    while offset < total_bits:
        bits = min(bits_per_step, total_bits - offset)
        items = [value]
        for digit in range(1, 1 << bits):
            pairs = [(source, source ^ (digit << offset)) for source in range(count)]
            items.append(lax.ppermute(value, axis, pairs))
        value = pairwise_total(items)
        offset += bits
    return value


def lane_gather_kernel(table_ref, index_ref, out_ref):
    out_ref[...] = jnp.take_along_axis(
        table_ref[...], index_ref[...], axis=1, mode="promise_in_bounds"
    )


def lane_gather(table, index):
    return pl.pallas_call(
        lane_gather_kernel,
        out_shape=jax.ShapeDtypeStruct(table.shape, table.dtype),
    )(table, index)


def lane_scatter_kernel(value_ref, index_ref, out_ref):
    tiles = BLOCK // 8
    for lane_tile in range(out_ref.shape[1] // BLOCK):
        lanes = pl.ds(lane_tile * BLOCK, BLOCK)

        def step(group, sums):
            start = pl.multiple_of(group * 8, 8)
            values = value_ref[pl.ds(start, 8), lanes]
            indices = index_ref[pl.ds(start, 8), lanes]
            for sub in range(8):
                value = jnp.broadcast_to(values[sub : sub + 1, :], (8, BLOCK))
                index = jnp.broadcast_to(indices[sub : sub + 1, :], (8, BLOCK))
                sums = tuple(
                    sums[tile]
                    + jnp.where(
                        index == lax.broadcasted_iota(jnp.int32, (8, BLOCK), 0) + 8 * tile,
                        value,
                        0.0,
                    )
                    for tile in range(tiles)
                )
            return sums

        zero = jnp.zeros((8, BLOCK), jnp.float32)
        sums = lax.fori_loop(0, tiles, step, (zero,) * tiles)
        for tile in range(tiles):
            out_ref[pl.ds(tile * 8, 8), lanes] = sums[tile]


def lane_scatter(values, index):
    count = values.shape[0]
    padded = -(-count // BLOCK) * BLOCK
    values_t = jnp.pad(values, ((0, padded - count), (0, 0))).T
    index_t = jnp.pad(index, ((0, padded - count), (0, 0))).T
    out = pl.pallas_call(
        lane_scatter_kernel,
        out_shape=jax.ShapeDtypeStruct((BLOCK, padded), values.dtype),
    )(values_t, index_t)
    return out.T[:count]


def gather_blocks(table, blocks, rows):
    lead = table.shape[:-1]
    tiled = table.reshape(lead + (-1, BLOCK))
    picked = jnp.take(tiled, blocks, axis=-2)
    index = jnp.broadcast_to(rows.reshape(-1, BLOCK), picked.shape)
    values = lane_gather(picked.reshape(-1, BLOCK), index.reshape(-1, BLOCK))
    return values.reshape(lead + (-1,))


def scatter_blocks(values, blocks, rows, count):
    lead = values.shape[:-1]
    tiled = values.reshape(lead + (-1, BLOCK))
    index = jnp.broadcast_to(rows.reshape(-1, BLOCK), tiled.shape)
    within = lane_scatter(tiled.reshape(-1, BLOCK), index.reshape(-1, BLOCK))
    within = within.reshape(tiled.shape)
    out = jnp.zeros(lead + (count, BLOCK), values.dtype)
    out = out.at[..., blocks, :].add(within)
    return out.reshape(lead + (-1,))


def body(
    direction_nodal,
    direction_capacity,
    residual_nodal,
    residual_capacity,
    scale_flow,
    scale_dispatch,
    scale_storage,
    scale_capacity,
    availability,
    retention,
    line_anchor,
    line_target,
    anchor_rows,
    target_rows,
    column_block,
    column_rows,
):
    net_count = lax.axis_size("net")
    net_index = lax.axis_index("net")
    lines = anchor_rows.shape[0]

    partial_sums = -jnp.sum(availability[None] * direction_capacity, axis=1)

    balance = direction_nodal[:, :, 0, :]
    storage = direction_nodal[:, :, 1, :]
    buses = balance.shape[-1] * net_count
    if net_count == 2:
        other = lax.ppermute(balance, "net", [(0, 1), (1, 0)])
        network = jnp.where(
            net_index == 0,
            jnp.concatenate([balance, other], axis=-1),
            jnp.concatenate([other, balance], axis=-1),
        )
    else:
        network = lax.all_gather(balance, "net", axis=2, tiled=True)

    blocks = jnp.concatenate([line_anchor, line_target, column_block])
    rows = jnp.concatenate([anchor_rows, target_rows, column_rows])
    gathered = gather_blocks(network, blocks, rows)
    flow_value = gathered[..., :lines] - gathered[..., lines : 2 * lines]
    dispatch_value = gathered[..., 2 * lines :] + direction_capacity

    tm_count = lax.axis_size("tm")
    tm_index = lax.axis_index("tm")
    level_scale = scale_storage[None, :, 0, :]
    charge_value = balance - storage
    flow_scaled = scale_flow[None] * flow_value
    dispatch_scaled = scale_dispatch[None] * dispatch_value
    charge_scaled = scale_storage[None, :, 1, :] * charge_value
    squares_local = jnp.sum(residual_nodal * residual_nodal, axis=(1, 2, 3)) + jnp.sum(
        residual_capacity * residual_capacity, axis=(1, 2)
    )
    inner_level = storage[:, :-1, :] - retention * storage[:, 1:, :]

    curvature_local = (
        jnp.sum(flow_scaled * flow_value, axis=(1, 2))
        + jnp.sum(dispatch_scaled * dispatch_value, axis=(1, 2))
        + jnp.sum(charge_scaled * charge_value, axis=(1, 2))
        + jnp.sum(level_scale[:, :-1] * inner_level * inner_level, axis=(1, 2))
        + DAMPING
        * (
            jnp.sum(direction_nodal * direction_nodal, axis=(1, 2, 3))
            + jnp.sum(direction_capacity * direction_capacity, axis=(1, 2))
        )
    )
    columns = partial_sums.shape[-1]
    scalars = jnp.stack([squares_local, curvature_local], axis=-1)
    head = jnp.concatenate([partial_sums, jnp.pad(scalars, ((0, 0), (0, BLOCK - 2)))], axis=-1)
    first_row = storage[:, 0, :]
    last_row = storage[:, -1, :]
    last_scale = jnp.broadcast_to(level_scale[:, -1, :], last_row.shape)
    width = columns + BLOCK
    bus_count = first_row.shape[-1]
    if not tm_count & (tm_count - 1):
        group_first, group_last, group_scale = first_row, last_row, last_scale
        step = 1
        while step < tm_count:
            pairs = [(source, source ^ step) for source in range(tm_count)]
            message = jnp.concatenate([head, group_first, group_last, group_scale], axis=-1)
            received = lax.ppermute(message, "tm", pairs)
            if step == 1:
                received, first_row, last_row, last_scale = lax.optimization_barrier(
                    (received, first_row, last_row, last_scale)
                )
                next_first = passed_along(first_row, "tm", -1)
                before = passed_along(jnp.stack([last_row, last_scale]), "tm", 1)
            got_first = received[:, width : width + bus_count]
            got_last = received[:, width + bus_count : width + 2 * bus_count]
            got_scale = received[:, width + 2 * bus_count :]
            lower = (tm_index // step) % 2 == 0
            low_last = jnp.where(lower, group_last, got_last)
            low_scale = jnp.where(lower, group_scale, got_scale)
            high_first = jnp.where(lower, got_first, group_first)
            span = low_last - retention * high_first
            head = head + received[:, :width]
            head = head.at[:, columns + 1].add(jnp.sum(low_scale * span * span, axis=-1))
            group_first = jnp.where(lower, group_first, got_first)
            group_last = jnp.where(lower, got_last, group_last)
            group_scale = jnp.where(lower, got_scale, group_scale)
            step *= 2
        span = group_last - retention * group_first
        head = head.at[:, columns + 1].add(jnp.sum(group_scale * span * span, axis=-1))
        packed = head
        if tm_count == 1:
            next_first = first_row
            before = jnp.stack([last_row, last_scale])
        behind = before[1] * (before[0] - retention * first_row)
    else:
        next_first = passed_along(first_row, "tm", -1)
        span = last_row - retention * next_first
        boundary = jnp.sum(last_scale * span * span, axis=-1)
        packed = lax.psum(head.at[:, columns + 1].add(boundary), "tm")
        behind = None
    storage_next = jnp.concatenate([storage[:, 1:, :], next_first[:, None, :]], axis=1)
    level_value = storage - retention * storage_next
    level_scaled = level_scale * level_value
    if behind is None:
        behind = passed_along(level_scaled[:, -1, :], "tm", 1)
    capacity_value = packed[:, :columns]
    capacity_scaled = scale_capacity[None] * capacity_value
    capacity_part = jnp.sum(capacity_scaled * capacity_value, axis=1)
    sums = packed[:, columns : columns + 2] + jnp.stack(
        [jnp.zeros_like(capacity_part), capacity_part], axis=-1
    )
    image_limit = (
        dispatch_scaled
        - availability[None] * capacity_scaled[:, None, :]
        + DAMPING * direction_capacity
    )
    sums, image_limit = lax.optimization_barrier((sums, image_limit))
    totals = butterfly_sum(sums, "net")

    bus_terms = scatter_blocks(
        jnp.concatenate([flow_scaled, -flow_scaled, dispatch_scaled], axis=-1),
        blocks,
        rows,
        buses // BLOCK,
    )
    if net_count == 2:
        half = buses // 2
        mine = lax.dynamic_slice_in_dim(bus_terms, net_index * half, half, axis=-1)
        theirs = lax.dynamic_slice_in_dim(bus_terms, (1 - net_index) * half, half, axis=-1)
        own_terms = mine + lax.ppermute(theirs, "net", [(0, 1), (1, 0)])
    else:
        own_terms = lax.psum_scatter(bus_terms, "net", scatter_dimension=2, tiled=True)
    image_balance = own_terms + charge_scaled + DAMPING * balance
    level_before = jnp.concatenate([behind[:, None, :], level_scaled[:, :-1, :]], axis=1)
    image_storage = level_scaled - retention * level_before - charge_scaled + DAMPING * storage
    image_nodal = jnp.stack([image_balance, image_storage], axis=2)
    step_size = totals[:, 0] / totals[:, 1]
    updated_nodal = residual_nodal - step_size[:, None, None, None] * image_nodal
    updated_capacity = residual_capacity - step_size[:, None, None] * image_limit
    return (updated_nodal, updated_capacity)


def solution(mesh):
    in_specs = (
        P(None, "tm", None, "net"),
        P(None, "tm", "net"),
        P(None, "tm", None, "net"),
        P(None, "tm", "net"),
        P("tm", "net"),
        P("tm", "net"),
        P("tm", None, "net"),
        P("net"),
        P("tm", "net"),
        P("net"),
        P("net"),
        P("net"),
        P("net"),
        P("net"),
        P("net"),
        P("net"),
    )
    out_specs = (P(None, "tm", None, "net"), P(None, "tm", "net"))
    return jax.shard_map(body, mesh=mesh, in_specs=in_specs, out_specs=out_specs, check_vma=False)
```

```python
import jax
import jax.numpy as jnp
from jax import lax
from jax.experimental import pallas as pl
from jax.sharding import PartitionSpec as P

BLOCK = 128


DAMPING = 0.5


def passed_along(value, axis, steps):
    count = lax.axis_size(axis)
    pairs = [(source, (source + steps) % count) for source in range(count)]
    return lax.ppermute(value, axis, pairs)


def butterfly_sum(value, axis):
    count = lax.axis_size(axis)
    if count & (count - 1):
        return lax.psum(value, axis)
    step = 1
    while step < count:
        pairs = [(source, source ^ step) for source in range(count)]
        value = value + lax.ppermute(value, axis, pairs)
        step *= 2
    return value


def pairwise_total(items):
    while len(items) > 1:
        items = [items[i] + items[i + 1] for i in range(0, len(items), 2)]
    return items[0]


def group_sum(value, axis, bits_per_step):
    count = lax.axis_size(axis)
    if count & (count - 1):
        return lax.psum(value, axis)
    total_bits = count.bit_length() - 1
    offset = 0
    while offset < total_bits:
        bits = min(bits_per_step, total_bits - offset)
        items = [value]
        for digit in range(1, 1 << bits):
            pairs = [(source, source ^ (digit << offset)) for source in range(count)]
            items.append(lax.ppermute(value, axis, pairs))
        value = pairwise_total(items)
        offset += bits
    return value


def lane_gather_kernel(table_ref, index_ref, out_ref):
    out_ref[...] = jnp.take_along_axis(
        table_ref[...], index_ref[...], axis=1, mode="promise_in_bounds"
    )


def lane_gather(table, index):
    return pl.pallas_call(
        lane_gather_kernel,
        out_shape=jax.ShapeDtypeStruct(table.shape, table.dtype),
    )(table, index)


def lane_scatter_kernel(value_ref, index_ref, out_ref):
    tiles = BLOCK // 8
    for lane_tile in range(out_ref.shape[1] // BLOCK):
        lanes = pl.ds(lane_tile * BLOCK, BLOCK)

        def step(group, sums):
            start = pl.multiple_of(group * 8, 8)
            values = value_ref[pl.ds(start, 8), lanes]
            indices = index_ref[pl.ds(start, 8), lanes]
            for sub in range(8):
                value = jnp.broadcast_to(values[sub : sub + 1, :], (8, BLOCK))
                index = jnp.broadcast_to(indices[sub : sub + 1, :], (8, BLOCK))
                sums = tuple(
                    sums[tile]
                    + jnp.where(
                        index == lax.broadcasted_iota(jnp.int32, (8, BLOCK), 0) + 8 * tile,
                        value,
                        0.0,
                    )
                    for tile in range(tiles)
                )
            return sums

        zero = jnp.zeros((8, BLOCK), jnp.float32)
        sums = lax.fori_loop(0, tiles, step, (zero,) * tiles)
        for tile in range(tiles):
            out_ref[pl.ds(tile * 8, 8), lanes] = sums[tile]


def lane_scatter(values, index):
    count = values.shape[0]
    padded = -(-count // BLOCK) * BLOCK
    values_t = jnp.pad(values, ((0, padded - count), (0, 0))).T
    index_t = jnp.pad(index, ((0, padded - count), (0, 0))).T
    out = pl.pallas_call(
        lane_scatter_kernel,
        out_shape=jax.ShapeDtypeStruct((BLOCK, padded), values.dtype),
    )(values_t, index_t)
    return out.T[:count]


def gather_blocks(table, blocks, rows):
    lead = table.shape[:-1]
    tiled = table.reshape(lead + (-1, BLOCK))
    picked = jnp.take(tiled, blocks, axis=-2)
    index = jnp.broadcast_to(rows.reshape(-1, BLOCK), picked.shape)
    values = lane_gather(picked.reshape(-1, BLOCK), index.reshape(-1, BLOCK))
    return values.reshape(lead + (-1,))


def scatter_blocks(values, blocks, rows, count):
    lead = values.shape[:-1]
    tiled = values.reshape(lead + (-1, BLOCK))
    index = jnp.broadcast_to(rows.reshape(-1, BLOCK), tiled.shape)
    within = lane_scatter(tiled.reshape(-1, BLOCK), index.reshape(-1, BLOCK))
    within = within.reshape(tiled.shape)
    out = jnp.zeros(lead + (count, BLOCK), values.dtype)
    out = out.at[..., blocks, :].add(within)
    return out.reshape(lead + (-1,))


def body(
    direction_nodal,
    direction_capacity,
    residual_nodal,
    residual_capacity,
    scale_flow,
    scale_dispatch,
    scale_storage,
    scale_capacity,
    availability,
    retention,
    line_anchor,
    line_target,
    anchor_rows,
    target_rows,
    column_block,
    column_rows,
):
    net_count = lax.axis_size("net")
    net_index = lax.axis_index("net")
    lines = anchor_rows.shape[0]

    partial_sums = -jnp.sum(availability[None] * direction_capacity, axis=1)

    balance = direction_nodal[:, :, 0, :]
    storage = direction_nodal[:, :, 1, :]
    buses = balance.shape[-1] * net_count
    if net_count == 2:
        other = lax.ppermute(balance, "net", [(0, 1), (1, 0)])
        network = jnp.where(
            net_index == 0,
            jnp.concatenate([balance, other], axis=-1),
            jnp.concatenate([other, balance], axis=-1),
        )
    else:
        network = lax.all_gather(balance, "net", axis=2, tiled=True)

    blocks = jnp.concatenate([line_anchor, line_target, column_block])
    rows = jnp.concatenate([anchor_rows, target_rows, column_rows])
    gathered = gather_blocks(network, blocks, rows)
    flow_value = gathered[..., :lines] - gathered[..., lines : 2 * lines]
    dispatch_value = gathered[..., 2 * lines :] + direction_capacity

    first_hour, gathered = lax.optimization_barrier((storage[:, :1], gathered))
    next_first = passed_along(first_hour, "tm", -1)
    storage_next = jnp.concatenate([storage[:, 1:, :], next_first], axis=1)
    level_value = storage - retention * storage_next
    charge_value = balance - storage
    flow_scaled = scale_flow[None] * flow_value
    dispatch_scaled = scale_dispatch[None] * dispatch_value
    level_scaled = scale_storage[None, :, 0, :] * level_value
    charge_scaled = scale_storage[None, :, 1, :] * charge_value
    squares_local = jnp.sum(residual_nodal * residual_nodal, axis=(1, 2, 3)) + jnp.sum(
        residual_capacity * residual_capacity, axis=(1, 2)
    )

    curvature_local = (
        jnp.sum(flow_scaled * flow_value, axis=(1, 2))
        + jnp.sum(
            dispatch_scaled * dispatch_value + DAMPING * direction_capacity * direction_capacity,
            axis=(1, 2),
        )
        + jnp.sum(
            charge_scaled * charge_value
            + level_scaled * level_value
            + DAMPING * (balance * balance + storage * storage),
            axis=(1, 2),
        )
    )
    columns = partial_sums.shape[-1]
    scalars = jnp.stack([squares_local, curvature_local], axis=-1)
    packed = jnp.concatenate(
        [partial_sums, jnp.pad(scalars, ((0, 0), (0, BLOCK - 2)))], axis=-1
    )
    packed = butterfly_sum(packed, "tm")
    capacity_value = packed[:, :columns]
    capacity_scaled = scale_capacity[None] * capacity_value
    capacity_part = jnp.sum(capacity_scaled * capacity_value, axis=1)
    sums = packed[:, columns : columns + 2] + jnp.stack(
        [jnp.zeros_like(capacity_part), capacity_part], axis=-1
    )
    image_limit = (
        dispatch_scaled
        - availability[None] * capacity_scaled[:, None, :]
        + DAMPING * direction_capacity
    )
    sums, image_limit = lax.optimization_barrier((sums, image_limit))
    totals = butterfly_sum(sums, "net")

    bus_terms = scatter_blocks(
        jnp.concatenate([flow_scaled, -flow_scaled, dispatch_scaled], axis=-1),
        blocks,
        rows,
        buses // BLOCK,
    )
    if net_count == 2:
        half = buses // 2
        mine = lax.dynamic_slice_in_dim(bus_terms, net_index * half, half, axis=-1)
        theirs = lax.dynamic_slice_in_dim(bus_terms, (1 - net_index) * half, half, axis=-1)
        own_terms = mine + lax.ppermute(theirs, "net", [(0, 1), (1, 0)])
    else:
        own_terms = lax.psum_scatter(bus_terms, "net", scatter_dimension=2, tiled=True)
    image_balance = own_terms + charge_scaled + DAMPING * balance
    behind = passed_along(level_scaled[:, -1:], "tm", 1)
    level_before = jnp.concatenate([behind, level_scaled[:, :-1, :]], axis=1)
    image_storage = level_scaled - retention * level_before - charge_scaled + DAMPING * storage
    image_nodal = jnp.stack([image_balance, image_storage], axis=2)
    step_size = totals[:, 0] / totals[:, 1]
    updated_nodal = residual_nodal - step_size[:, None, None, None] * image_nodal
    updated_capacity = residual_capacity - step_size[:, None, None] * image_limit
    return (updated_nodal, updated_capacity)


def solution(mesh):
    in_specs = (
        P(None, "tm", None, "net"),
        P(None, "tm", "net"),
        P(None, "tm", None, "net"),
        P(None, "tm", "net"),
        P("tm", "net"),
        P("tm", "net"),
        P("tm", None, "net"),
        P("net"),
        P("tm", "net"),
        P("net"),
        P("net"),
        P("net"),
        P("net"),
        P("net"),
        P("net"),
        P("net"),
    )
    out_specs = (P(None, "tm", None, "net"), P(None, "tm", "net"))
    return jax.shard_map(body, mesh=mesh, in_specs=in_specs, out_specs=out_specs, check_vma=False)
```

```python
import jax
import jax.numpy as jnp
from jax import lax
from jax.experimental import pallas as pl
from jax.sharding import PartitionSpec as P

BLOCK = 128


DAMPING = 0.5


def passed_along(value, axis, steps):
    count = lax.axis_size(axis)
    pairs = [(source, (source + steps) % count) for source in range(count)]
    return lax.ppermute(value, axis, pairs)


def butterfly_sum(value, axis):
    count = lax.axis_size(axis)
    if count & (count - 1):
        return lax.psum(value, axis)
    step = 1
    while step < count:
        pairs = [(source, source ^ step) for source in range(count)]
        value = value + lax.ppermute(value, axis, pairs)
        step *= 2
    return value


def pairwise_total(items):
    while len(items) > 1:
        items = [items[i] + items[i + 1] for i in range(0, len(items), 2)]
    return items[0]


def group_sum(value, axis, bits_per_step):
    count = lax.axis_size(axis)
    if count & (count - 1):
        return lax.psum(value, axis)
    total_bits = count.bit_length() - 1
    offset = 0
    while offset < total_bits:
        bits = min(bits_per_step, total_bits - offset)
        items = [value]
        for digit in range(1, 1 << bits):
            pairs = [(source, source ^ (digit << offset)) for source in range(count)]
            items.append(lax.ppermute(value, axis, pairs))
        value = pairwise_total(items)
        offset += bits
    return value


def lane_gather_kernel(table_ref, index_ref, out_ref):
    out_ref[...] = jnp.take_along_axis(
        table_ref[...], index_ref[...], axis=1, mode="promise_in_bounds"
    )


def lane_gather(table, index):
    return pl.pallas_call(
        lane_gather_kernel,
        out_shape=jax.ShapeDtypeStruct(table.shape, table.dtype),
    )(table, index)


def lane_scatter_kernel(value_ref, index_ref, out_ref):
    tiles = BLOCK // 8
    for lane_tile in range(out_ref.shape[1] // BLOCK):
        lanes = pl.ds(lane_tile * BLOCK, BLOCK)

        def step(group, sums):
            start = pl.multiple_of(group * 8, 8)
            values = value_ref[pl.ds(start, 8), lanes]
            indices = index_ref[pl.ds(start, 8), lanes]
            for sub in range(8):
                value = jnp.broadcast_to(values[sub : sub + 1, :], (8, BLOCK))
                index = jnp.broadcast_to(indices[sub : sub + 1, :], (8, BLOCK))
                sums = tuple(
                    sums[tile]
                    + jnp.where(
                        index == lax.broadcasted_iota(jnp.int32, (8, BLOCK), 0) + 8 * tile,
                        value,
                        0.0,
                    )
                    for tile in range(tiles)
                )
            return sums

        zero = jnp.zeros((8, BLOCK), jnp.float32)
        sums = lax.fori_loop(0, tiles, step, (zero,) * tiles)
        for tile in range(tiles):
            out_ref[pl.ds(tile * 8, 8), lanes] = sums[tile]


def lane_scatter(values, index):
    count = values.shape[0]
    padded = -(-count // BLOCK) * BLOCK
    values_t = jnp.pad(values, ((0, padded - count), (0, 0))).T
    index_t = jnp.pad(index, ((0, padded - count), (0, 0))).T
    out = pl.pallas_call(
        lane_scatter_kernel,
        out_shape=jax.ShapeDtypeStruct((BLOCK, padded), values.dtype),
    )(values_t, index_t)
    return out.T[:count]


def gather_blocks(table, blocks, rows):
    lead = table.shape[:-1]
    tiled = table.reshape(lead + (-1, BLOCK))
    picked = jnp.take(tiled, blocks, axis=-2)
    index = jnp.broadcast_to(rows.reshape(-1, BLOCK), picked.shape)
    values = lane_gather(picked.reshape(-1, BLOCK), index.reshape(-1, BLOCK))
    return values.reshape(lead + (-1,))


def scatter_blocks(values, blocks, rows, count):
    lead = values.shape[:-1]
    tiled = values.reshape(lead + (-1, BLOCK))
    index = jnp.broadcast_to(rows.reshape(-1, BLOCK), tiled.shape)
    within = lane_scatter(tiled.reshape(-1, BLOCK), index.reshape(-1, BLOCK))
    within = within.reshape(tiled.shape)
    out = jnp.zeros(lead + (count, BLOCK), values.dtype)
    out = out.at[..., blocks, :].add(within)
    return out.reshape(lead + (-1,))


def body(
    direction_nodal,
    direction_capacity,
    residual_nodal,
    residual_capacity,
    scale_flow,
    scale_dispatch,
    scale_storage,
    scale_capacity,
    availability,
    retention,
    line_anchor,
    line_target,
    anchor_rows,
    target_rows,
    column_block,
    column_rows,
):
    net_count = lax.axis_size("net")
    net_index = lax.axis_index("net")
    lines = anchor_rows.shape[0]

    partial_sums = -jnp.sum(availability[None] * direction_capacity, axis=1)

    balance = direction_nodal[:, :, 0, :]
    storage = direction_nodal[:, :, 1, :]
    buses = balance.shape[-1] * net_count
    if net_count == 2:
        other = lax.ppermute(balance, "net", [(0, 1), (1, 0)])
        network = jnp.where(
            net_index == 0,
            jnp.concatenate([balance, other], axis=-1),
            jnp.concatenate([other, balance], axis=-1),
        )
    else:
        network = lax.all_gather(balance, "net", axis=2, tiled=True)

    blocks = jnp.concatenate([line_anchor, line_target, column_block])
    rows = jnp.concatenate([anchor_rows, target_rows, column_rows])
    gathered = gather_blocks(network, blocks, rows)
    flow_value = gathered[..., :lines] - gathered[..., lines : 2 * lines]
    dispatch_value = gathered[..., 2 * lines :] + direction_capacity

    next_first = passed_along(storage[:, :1], "tm", -1)
    storage_next = jnp.concatenate([storage[:, 1:, :], next_first], axis=1)
    level_value = storage - retention * storage_next
    charge_value = balance - storage
    flow_scaled = scale_flow[None] * flow_value
    dispatch_scaled = scale_dispatch[None] * dispatch_value
    level_scaled = scale_storage[None, :, 0, :] * level_value
    charge_scaled = scale_storage[None, :, 1, :] * charge_value
    squares_local = jnp.sum(residual_nodal * residual_nodal, axis=(1, 2, 3)) + jnp.sum(
        residual_capacity * residual_capacity, axis=(1, 2)
    )

    curvature_local = (
        jnp.sum(flow_scaled * flow_value, axis=(1, 2))
        + jnp.sum(
            dispatch_scaled * dispatch_value + DAMPING * direction_capacity * direction_capacity,
            axis=(1, 2),
        )
        + jnp.sum(
            charge_scaled * charge_value
            + level_scaled * level_value
            + DAMPING * (balance * balance + storage * storage),
            axis=(1, 2),
        )
    )
    columns = partial_sums.shape[-1]
    scalars = jnp.stack([squares_local, curvature_local], axis=-1)
    packed = jnp.concatenate(
        [partial_sums, jnp.pad(scalars, ((0, 0), (0, BLOCK - 2)))], axis=-1
    )
    packed = butterfly_sum(packed, "tm")
    capacity_value = packed[:, :columns]
    capacity_scaled = scale_capacity[None] * capacity_value
    capacity_part = jnp.sum(capacity_scaled * capacity_value, axis=1)
    sums = packed[:, columns : columns + 2] + jnp.stack(
        [jnp.zeros_like(capacity_part), capacity_part], axis=-1
    )
    image_limit = (
        dispatch_scaled
        - availability[None] * capacity_scaled[:, None, :]
        + DAMPING * direction_capacity
    )
    bus_terms = scatter_blocks(
        jnp.concatenate([flow_scaled, -flow_scaled, dispatch_scaled], axis=-1),
        blocks,
        rows,
        buses // BLOCK,
    )
    if net_count == 2:
        half = buses // 2
        mine = lax.dynamic_slice_in_dim(bus_terms, net_index * half, half, axis=-1)
        theirs = lax.dynamic_slice_in_dim(bus_terms, (1 - net_index) * half, half, axis=-1)
        own_terms = mine + lax.ppermute(theirs, "net", [(0, 1), (1, 0)])
    else:
        own_terms = lax.psum_scatter(bus_terms, "net", scatter_dimension=2, tiled=True)
    image_balance = own_terms + charge_scaled + DAMPING * balance
    behind = passed_along(level_scaled[:, -1:], "tm", 1)
    level_before = jnp.concatenate([behind, level_scaled[:, :-1, :]], axis=1)
    image_storage = level_scaled - retention * level_before - charge_scaled + DAMPING * storage
    image_nodal = jnp.stack([image_balance, image_storage], axis=2)
    sums, image_limit, image_nodal = lax.optimization_barrier((sums, image_limit, image_nodal))
    totals = butterfly_sum(sums, "net")

    step_size = totals[:, 0] / totals[:, 1]
    updated_nodal = residual_nodal - step_size[:, None, None, None] * image_nodal
    updated_capacity = residual_capacity - step_size[:, None, None] * image_limit
    return (updated_nodal, updated_capacity)


def solution(mesh):
    in_specs = (
        P(None, "tm", None, "net"),
        P(None, "tm", "net"),
        P(None, "tm", None, "net"),
        P(None, "tm", "net"),
        P("tm", "net"),
        P("tm", "net"),
        P("tm", None, "net"),
        P("net"),
        P("tm", "net"),
        P("net"),
        P("net"),
        P("net"),
        P("net"),
        P("net"),
        P("net"),
        P("net"),
    )
    out_specs = (P(None, "tm", None, "net"), P(None, "tm", "net"))
    return jax.shard_map(body, mesh=mesh, in_specs=in_specs, out_specs=out_specs, check_vma=False)
```

```python
import jax
import jax.numpy as jnp
from jax import lax
from jax.experimental import pallas as pl
from jax.sharding import PartitionSpec as P

BLOCK = 128


DAMPING = 0.5


def passed_along(value, axis, steps):
    count = lax.axis_size(axis)
    pairs = [(source, (source + steps) % count) for source in range(count)]
    return lax.ppermute(value, axis, pairs)


def butterfly_masks(count):
    masks = [1 << bit for bit in range(count.bit_length() - 1)]
    if count == 128:
        masks[2] = 6
        masks[6] = 96
    return masks


def butterfly_sum(value, axis):
    count = lax.axis_size(axis)
    if count & (count - 1):
        return lax.psum(value, axis)
    for mask in butterfly_masks(count):
        pairs = [(source, source ^ mask) for source in range(count)]
        value = value + lax.ppermute(value, axis, pairs)
    return value


def pairwise_total(items):
    while len(items) > 1:
        items = [items[i] + items[i + 1] for i in range(0, len(items), 2)]
    return items[0]


def group_sum(value, axis, bits_per_step):
    count = lax.axis_size(axis)
    if count & (count - 1):
        return lax.psum(value, axis)
    total_bits = count.bit_length() - 1
    offset = 0
    while offset < total_bits:
        bits = min(bits_per_step, total_bits - offset)
        items = [value]
        for digit in range(1, 1 << bits):
            pairs = [(source, source ^ (digit << offset)) for source in range(count)]
            items.append(lax.ppermute(value, axis, pairs))
        value = pairwise_total(items)
        offset += bits
    return value


def lane_gather_kernel(table_ref, index_ref, out_ref):
    out_ref[...] = jnp.take_along_axis(
        table_ref[...], index_ref[...], axis=1, mode="promise_in_bounds"
    )


def lane_gather(table, index):
    return pl.pallas_call(
        lane_gather_kernel,
        out_shape=jax.ShapeDtypeStruct(table.shape, table.dtype),
    )(table, index)


def lane_scatter_kernel(value_ref, index_ref, out_ref):
    tiles = BLOCK // 8
    for lane_tile in range(out_ref.shape[1] // BLOCK):
        lanes = pl.ds(lane_tile * BLOCK, BLOCK)

        def step(group, sums):
            start = pl.multiple_of(group * 8, 8)
            values = value_ref[pl.ds(start, 8), lanes]
            indices = index_ref[pl.ds(start, 8), lanes]
            for sub in range(8):
                value = jnp.broadcast_to(values[sub : sub + 1, :], (8, BLOCK))
                index = jnp.broadcast_to(indices[sub : sub + 1, :], (8, BLOCK))
                sums = tuple(
                    sums[tile]
                    + jnp.where(
                        index == lax.broadcasted_iota(jnp.int32, (8, BLOCK), 0) + 8 * tile,
                        value,
                        0.0,
                    )
                    for tile in range(tiles)
                )
            return sums

        zero = jnp.zeros((8, BLOCK), jnp.float32)
        sums = lax.fori_loop(0, tiles, step, (zero,) * tiles)
        for tile in range(tiles):
            out_ref[pl.ds(tile * 8, 8), lanes] = sums[tile]


def lane_scatter(values, index):
    count = values.shape[0]
    padded = -(-count // BLOCK) * BLOCK
    values_t = jnp.pad(values, ((0, padded - count), (0, 0))).T
    index_t = jnp.pad(index, ((0, padded - count), (0, 0))).T
    out = pl.pallas_call(
        lane_scatter_kernel,
        out_shape=jax.ShapeDtypeStruct((BLOCK, padded), values.dtype),
    )(values_t, index_t)
    return out.T[:count]


def gather_blocks(table, blocks, rows):
    lead = table.shape[:-1]
    tiled = table.reshape(lead + (-1, BLOCK))
    picked = jnp.take(tiled, blocks, axis=-2)
    index = jnp.broadcast_to(rows.reshape(-1, BLOCK), picked.shape)
    values = lane_gather(picked.reshape(-1, BLOCK), index.reshape(-1, BLOCK))
    return values.reshape(lead + (-1,))


def scatter_blocks(values, blocks, rows, count):
    lead = values.shape[:-1]
    tiled = values.reshape(lead + (-1, BLOCK))
    index = jnp.broadcast_to(rows.reshape(-1, BLOCK), tiled.shape)
    within = lane_scatter(tiled.reshape(-1, BLOCK), index.reshape(-1, BLOCK))
    within = within.reshape(tiled.shape)
    out = jnp.zeros(lead + (count, BLOCK), values.dtype)
    out = out.at[..., blocks, :].add(within)
    return out.reshape(lead + (-1,))


def body(
    direction_nodal,
    direction_capacity,
    residual_nodal,
    residual_capacity,
    scale_flow,
    scale_dispatch,
    scale_storage,
    scale_capacity,
    availability,
    retention,
    line_anchor,
    line_target,
    anchor_rows,
    target_rows,
    column_block,
    column_rows,
):
    net_count = lax.axis_size("net")
    net_index = lax.axis_index("net")
    lines = anchor_rows.shape[0]

    partial_sums = -jnp.sum(availability[None] * direction_capacity, axis=1)

    balance = direction_nodal[:, :, 0, :]
    storage = direction_nodal[:, :, 1, :]
    buses = balance.shape[-1] * net_count
    if net_count == 2:
        other = lax.ppermute(balance, "net", [(0, 1), (1, 0)])
        network = jnp.where(
            net_index == 0,
            jnp.concatenate([balance, other], axis=-1),
            jnp.concatenate([other, balance], axis=-1),
        )
    else:
        network = lax.all_gather(balance, "net", axis=2, tiled=True)

    blocks = jnp.concatenate([line_anchor, line_target, column_block])
    rows = jnp.concatenate([anchor_rows, target_rows, column_rows])
    gathered = gather_blocks(network, blocks, rows)
    flow_value = gathered[..., :lines] - gathered[..., lines : 2 * lines]
    dispatch_value = gathered[..., 2 * lines :] + direction_capacity

    first_hour, gathered = lax.optimization_barrier((storage[:, :1], gathered))
    next_first = passed_along(first_hour, "tm", -1)
    storage_next = jnp.concatenate([storage[:, 1:, :], next_first], axis=1)
    level_value = storage - retention * storage_next
    charge_value = balance - storage
    flow_scaled = scale_flow[None] * flow_value
    dispatch_scaled = scale_dispatch[None] * dispatch_value
    level_scaled = scale_storage[None, :, 0, :] * level_value
    charge_scaled = scale_storage[None, :, 1, :] * charge_value
    squares_local = jnp.sum(residual_nodal * residual_nodal, axis=(1, 2, 3)) + jnp.sum(
        residual_capacity * residual_capacity, axis=(1, 2)
    )

    curvature_local = (
        jnp.sum(flow_scaled * flow_value, axis=(1, 2))
        + jnp.sum(
            dispatch_scaled * dispatch_value + DAMPING * direction_capacity * direction_capacity,
            axis=(1, 2),
        )
        + jnp.sum(
            charge_scaled * charge_value
            + level_scaled * level_value
            + DAMPING * (balance * balance + storage * storage),
            axis=(1, 2),
        )
    )
    columns = partial_sums.shape[-1]
    scalars = jnp.stack([squares_local, curvature_local], axis=-1)
    packed = jnp.concatenate(
        [partial_sums, jnp.pad(scalars, ((0, 0), (0, BLOCK - 2)))], axis=-1
    )
    packed = butterfly_sum(packed, "tm")
    capacity_value = packed[:, :columns]
    capacity_scaled = scale_capacity[None] * capacity_value
    capacity_part = jnp.sum(capacity_scaled * capacity_value, axis=1)
    sums = packed[:, columns : columns + 2] + jnp.stack(
        [jnp.zeros_like(capacity_part), capacity_part], axis=-1
    )
    image_limit = (
        dispatch_scaled
        - availability[None] * capacity_scaled[:, None, :]
        + DAMPING * direction_capacity
    )
    sums, image_limit = lax.optimization_barrier((sums, image_limit))
    totals = butterfly_sum(sums, "net")

    bus_terms = scatter_blocks(
        jnp.concatenate([flow_scaled, -flow_scaled, dispatch_scaled], axis=-1),
        blocks,
        rows,
        buses // BLOCK,
    )
    if net_count == 2:
        half = buses // 2
        mine = lax.dynamic_slice_in_dim(bus_terms, net_index * half, half, axis=-1)
        theirs = lax.dynamic_slice_in_dim(bus_terms, (1 - net_index) * half, half, axis=-1)
        own_terms = mine + lax.ppermute(theirs, "net", [(0, 1), (1, 0)])
    else:
        own_terms = lax.psum_scatter(bus_terms, "net", scatter_dimension=2, tiled=True)
    image_balance = own_terms + charge_scaled + DAMPING * balance
    behind = passed_along(level_scaled[:, -1:], "tm", 1)
    level_before = jnp.concatenate([behind, level_scaled[:, :-1, :]], axis=1)
    image_storage = level_scaled - retention * level_before - charge_scaled + DAMPING * storage
    image_nodal = jnp.stack([image_balance, image_storage], axis=2)
    step_size = totals[:, 0] / totals[:, 1]
    updated_nodal = residual_nodal - step_size[:, None, None, None] * image_nodal
    updated_capacity = residual_capacity - step_size[:, None, None] * image_limit
    return (updated_nodal, updated_capacity)


def solution(mesh):
    in_specs = (
        P(None, "tm", None, "net"),
        P(None, "tm", "net"),
        P(None, "tm", None, "net"),
        P(None, "tm", "net"),
        P("tm", "net"),
        P("tm", "net"),
        P("tm", None, "net"),
        P("net"),
        P("tm", "net"),
        P("net"),
        P("net"),
        P("net"),
        P("net"),
        P("net"),
        P("net"),
        P("net"),
    )
    out_specs = (P(None, "tm", None, "net"), P(None, "tm", "net"))
    return jax.shard_map(body, mesh=mesh, in_specs=in_specs, out_specs=out_specs, check_vma=False)
```

```python
import jax
import jax.numpy as jnp
from jax import lax
from jax.experimental import pallas as pl
from jax.sharding import PartitionSpec as P

BLOCK = 128


DAMPING = 0.5


def passed_along(value, axis, steps):
    count = lax.axis_size(axis)
    pairs = [(source, (source + steps) % count) for source in range(count)]
    return lax.ppermute(value, axis, pairs)


def tm_count_is_power(count):
    return count & (count - 1) == 0


def butterfly_masks(count):
    masks = [1 << bit for bit in range(count.bit_length() - 1)]
    if count == 128:
        masks[2] = 6
        masks[6] = 96
    return masks


def butterfly_sum(value, axis):
    count = lax.axis_size(axis)
    if count & (count - 1):
        return lax.psum(value, axis)
    for mask in butterfly_masks(count):
        pairs = [(source, source ^ mask) for source in range(count)]
        value = value + lax.ppermute(value, axis, pairs)
    return value


def pairwise_total(items):
    while len(items) > 1:
        items = [items[i] + items[i + 1] for i in range(0, len(items), 2)]
    return items[0]


def group_sum(value, axis, bits_per_step):
    count = lax.axis_size(axis)
    if count & (count - 1):
        return lax.psum(value, axis)
    total_bits = count.bit_length() - 1
    offset = 0
    while offset < total_bits:
        bits = min(bits_per_step, total_bits - offset)
        items = [value]
        for digit in range(1, 1 << bits):
            pairs = [(source, source ^ (digit << offset)) for source in range(count)]
            items.append(lax.ppermute(value, axis, pairs))
        value = pairwise_total(items)
        offset += bits
    return value


def lane_gather_kernel(table_ref, index_ref, out_ref):
    out_ref[...] = jnp.take_along_axis(
        table_ref[...], index_ref[...], axis=1, mode="promise_in_bounds"
    )


def lane_gather(table, index):
    return pl.pallas_call(
        lane_gather_kernel,
        out_shape=jax.ShapeDtypeStruct(table.shape, table.dtype),
    )(table, index)


def lane_scatter_kernel(value_ref, index_ref, out_ref):
    tiles = BLOCK // 8
    for lane_tile in range(out_ref.shape[1] // BLOCK):
        lanes = pl.ds(lane_tile * BLOCK, BLOCK)

        def step(group, sums):
            start = pl.multiple_of(group * 8, 8)
            values = value_ref[pl.ds(start, 8), lanes]
            indices = index_ref[pl.ds(start, 8), lanes]
            for sub in range(8):
                value = jnp.broadcast_to(values[sub : sub + 1, :], (8, BLOCK))
                index = jnp.broadcast_to(indices[sub : sub + 1, :], (8, BLOCK))
                sums = tuple(
                    sums[tile]
                    + jnp.where(
                        index == lax.broadcasted_iota(jnp.int32, (8, BLOCK), 0) + 8 * tile,
                        value,
                        0.0,
                    )
                    for tile in range(tiles)
                )
            return sums

        zero = jnp.zeros((8, BLOCK), jnp.float32)
        sums = lax.fori_loop(0, tiles, step, (zero,) * tiles)
        for tile in range(tiles):
            out_ref[pl.ds(tile * 8, 8), lanes] = sums[tile]


def lane_scatter(values, index):
    count = values.shape[0]
    padded = -(-count // BLOCK) * BLOCK
    values_t = jnp.pad(values, ((0, padded - count), (0, 0))).T
    index_t = jnp.pad(index, ((0, padded - count), (0, 0))).T
    out = pl.pallas_call(
        lane_scatter_kernel,
        out_shape=jax.ShapeDtypeStruct((BLOCK, padded), values.dtype),
    )(values_t, index_t)
    return out.T[:count]


def gather_blocks(table, blocks, rows):
    lead = table.shape[:-1]
    tiled = table.reshape(lead + (-1, BLOCK))
    picked = jnp.take(tiled, blocks, axis=-2)
    index = jnp.broadcast_to(rows.reshape(-1, BLOCK), picked.shape)
    values = lane_gather(picked.reshape(-1, BLOCK), index.reshape(-1, BLOCK))
    return values.reshape(lead + (-1,))


def scatter_blocks(values, blocks, rows, count):
    lead = values.shape[:-1]
    tiled = values.reshape(lead + (-1, BLOCK))
    index = jnp.broadcast_to(rows.reshape(-1, BLOCK), tiled.shape)
    within = lane_scatter(tiled.reshape(-1, BLOCK), index.reshape(-1, BLOCK))
    within = within.reshape(tiled.shape)
    out = jnp.zeros(lead + (count, BLOCK), values.dtype)
    out = out.at[..., blocks, :].add(within)
    return out.reshape(lead + (-1,))


def chain_with_fillers(value, axis, fillers):
    count = lax.axis_size(axis)
    state = None
    for index, mask in enumerate(butterfly_masks(count)):
        pairs = [(source, source ^ mask) for source in range(count)]
        if index in fillers:
            value, state = lax.optimization_barrier((value, state))
            state = fillers[index](state)
        value = value + lax.ppermute(value, axis, pairs)
        if index in fillers:
            value, state = lax.optimization_barrier((value, state))
    return value, state


def body(
    direction_nodal,
    direction_capacity,
    residual_nodal,
    residual_capacity,
    scale_flow,
    scale_dispatch,
    scale_storage,
    scale_capacity,
    availability,
    retention,
    line_anchor,
    line_target,
    anchor_rows,
    target_rows,
    column_block,
    column_rows,
):
    net_count = lax.axis_size("net")
    net_index = lax.axis_index("net")
    lines = anchor_rows.shape[0]

    partial_sums = -jnp.sum(availability[None] * direction_capacity, axis=1)

    balance = direction_nodal[:, :, 0, :]
    storage = direction_nodal[:, :, 1, :]
    buses = balance.shape[-1] * net_count
    if net_count == 2:
        other = lax.ppermute(balance, "net", [(0, 1), (1, 0)])
        network = jnp.where(
            net_index == 0,
            jnp.concatenate([balance, other], axis=-1),
            jnp.concatenate([other, balance], axis=-1),
        )
    else:
        network = lax.all_gather(balance, "net", axis=2, tiled=True)

    blocks = jnp.concatenate([line_anchor, line_target, column_block])
    rows = jnp.concatenate([anchor_rows, target_rows, column_rows])
    gathered = gather_blocks(network, blocks, rows)
    flow_value = gathered[..., :lines] - gathered[..., lines : 2 * lines]
    dispatch_value = gathered[..., 2 * lines :] + direction_capacity

    first_hour, gathered = lax.optimization_barrier((storage[:, :1], gathered))
    next_first = passed_along(first_hour, "tm", -1)
    storage_next = jnp.concatenate([storage[:, 1:, :], next_first], axis=1)
    level_value = storage - retention * storage_next
    charge_value = balance - storage
    flow_scaled = scale_flow[None] * flow_value
    dispatch_scaled = scale_dispatch[None] * dispatch_value
    level_scaled = scale_storage[None, :, 0, :] * level_value
    charge_scaled = scale_storage[None, :, 1, :] * charge_value
    squares_local = jnp.sum(residual_nodal * residual_nodal, axis=(1, 2, 3)) + jnp.sum(
        residual_capacity * residual_capacity, axis=(1, 2)
    )

    curvature_local = (
        jnp.sum(flow_scaled * flow_value, axis=(1, 2))
        + jnp.sum(
            dispatch_scaled * dispatch_value + DAMPING * direction_capacity * direction_capacity,
            axis=(1, 2),
        )
        + jnp.sum(
            charge_scaled * charge_value
            + level_scaled * level_value
            + DAMPING * (balance * balance + storage * storage),
            axis=(1, 2),
        )
    )
    columns = partial_sums.shape[-1]
    scalars = jnp.stack([squares_local, curvature_local], axis=-1)
    packed = jnp.concatenate(
        [partial_sums, jnp.pad(scalars, ((0, 0), (0, BLOCK - 2)))], axis=-1
    )
    scatter_values = jnp.concatenate([flow_scaled, -flow_scaled, dispatch_scaled], axis=-1)
    lead = scatter_values.shape[:-1]
    tiled = scatter_values.reshape(lead + (-1, BLOCK))
    scatter_index = jnp.broadcast_to(rows.reshape(-1, BLOCK), tiled.shape)

    def within_blocks(state):
        return lane_scatter(tiled.reshape(-1, BLOCK), scatter_index.reshape(-1, BLOCK))

    def onto_buses(within):
        out = jnp.zeros(lead + (buses // BLOCK, BLOCK), tiled.dtype)
        return out.at[..., blocks, :].add(within.reshape(tiled.shape)).reshape(lead + (-1,))

    steps = lax.axis_size("tm").bit_length() - 1
    if tm_count_is_power(lax.axis_size("tm")) and steps >= 3:
        first = min(2, steps - 2)
        packed, bus_terms = chain_with_fillers(
            packed, "tm", {first: within_blocks, first + 1: onto_buses}
        )
    else:
        packed = butterfly_sum(packed, "tm")
        bus_terms = onto_buses(within_blocks(None))
    capacity_value = packed[:, :columns]
    capacity_scaled = scale_capacity[None] * capacity_value
    capacity_part = jnp.sum(capacity_scaled * capacity_value, axis=1)
    sums = packed[:, columns : columns + 2] + jnp.stack(
        [jnp.zeros_like(capacity_part), capacity_part], axis=-1
    )
    image_limit = (
        dispatch_scaled
        - availability[None] * capacity_scaled[:, None, :]
        + DAMPING * direction_capacity
    )
    sums, image_limit = lax.optimization_barrier((sums, image_limit))
    totals = butterfly_sum(sums, "net")

    if net_count == 2:
        half = buses // 2
        mine = lax.dynamic_slice_in_dim(bus_terms, net_index * half, half, axis=-1)
        theirs = lax.dynamic_slice_in_dim(bus_terms, (1 - net_index) * half, half, axis=-1)
        own_terms = mine + lax.ppermute(theirs, "net", [(0, 1), (1, 0)])
    else:
        own_terms = lax.psum_scatter(bus_terms, "net", scatter_dimension=2, tiled=True)
    image_balance = own_terms + charge_scaled + DAMPING * balance
    behind = passed_along(level_scaled[:, -1:], "tm", 1)
    level_before = jnp.concatenate([behind, level_scaled[:, :-1, :]], axis=1)
    image_storage = level_scaled - retention * level_before - charge_scaled + DAMPING * storage
    image_nodal = jnp.stack([image_balance, image_storage], axis=2)
    step_size = totals[:, 0] / totals[:, 1]
    updated_nodal = residual_nodal - step_size[:, None, None, None] * image_nodal
    updated_capacity = residual_capacity - step_size[:, None, None] * image_limit
    return (updated_nodal, updated_capacity)


def solution(mesh):
    in_specs = (
        P(None, "tm", None, "net"),
        P(None, "tm", "net"),
        P(None, "tm", None, "net"),
        P(None, "tm", "net"),
        P("tm", "net"),
        P("tm", "net"),
        P("tm", None, "net"),
        P("net"),
        P("tm", "net"),
        P("net"),
        P("net"),
        P("net"),
        P("net"),
        P("net"),
        P("net"),
        P("net"),
    )
    out_specs = (P(None, "tm", None, "net"), P(None, "tm", "net"))
    return jax.shard_map(body, mesh=mesh, in_specs=in_specs, out_specs=out_specs, check_vma=False)
```

```python
import jax
import jax.numpy as jnp
from jax import lax
from jax.experimental import pallas as pl
from jax.sharding import PartitionSpec as P

BLOCK = 128


DAMPING = 0.5


def passed_along(value, axis, steps):
    count = lax.axis_size(axis)
    pairs = [(source, (source + steps) % count) for source in range(count)]
    return lax.ppermute(value, axis, pairs)


def tm_count_is_power(count):
    return count & (count - 1) == 0


def butterfly_masks(count):
    masks = [1 << bit for bit in range(count.bit_length() - 1)]
    if count == 128:
        masks[2] = 6
        masks[6] = 96
    return masks


def butterfly_sum(value, axis):
    count = lax.axis_size(axis)
    if count & (count - 1):
        return lax.psum(value, axis)
    for mask in butterfly_masks(count):
        pairs = [(source, source ^ mask) for source in range(count)]
        value = value + lax.ppermute(value, axis, pairs)
    return value


def pairwise_total(items):
    while len(items) > 1:
        items = [items[i] + items[i + 1] for i in range(0, len(items), 2)]
    return items[0]


def group_sum(value, axis, bits_per_step):
    count = lax.axis_size(axis)
    if count & (count - 1):
        return lax.psum(value, axis)
    total_bits = count.bit_length() - 1
    offset = 0
    while offset < total_bits:
        bits = min(bits_per_step, total_bits - offset)
        items = [value]
        for digit in range(1, 1 << bits):
            pairs = [(source, source ^ (digit << offset)) for source in range(count)]
            items.append(lax.ppermute(value, axis, pairs))
        value = pairwise_total(items)
        offset += bits
    return value


def lane_gather_kernel(table_ref, index_ref, out_ref):
    out_ref[...] = jnp.take_along_axis(
        table_ref[...], index_ref[...], axis=1, mode="promise_in_bounds"
    )


def lane_gather(table, index):
    return pl.pallas_call(
        lane_gather_kernel,
        out_shape=jax.ShapeDtypeStruct(table.shape, table.dtype),
    )(table, index)


def lane_scatter_kernel(value_ref, index_ref, out_ref):
    tiles = BLOCK // 8
    for lane_tile in range(out_ref.shape[1] // BLOCK):
        lanes = pl.ds(lane_tile * BLOCK, BLOCK)

        def step(group, sums):
            start = pl.multiple_of(group * 8, 8)
            values = value_ref[pl.ds(start, 8), lanes]
            indices = index_ref[pl.ds(start, 8), lanes]
            for sub in range(8):
                value = jnp.broadcast_to(values[sub : sub + 1, :], (8, BLOCK))
                index = jnp.broadcast_to(indices[sub : sub + 1, :], (8, BLOCK))
                sums = tuple(
                    sums[tile]
                    + jnp.where(
                        index == lax.broadcasted_iota(jnp.int32, (8, BLOCK), 0) + 8 * tile,
                        value,
                        0.0,
                    )
                    for tile in range(tiles)
                )
            return sums

        zero = jnp.zeros((8, BLOCK), jnp.float32)
        sums = lax.fori_loop(0, tiles, step, (zero,) * tiles)
        for tile in range(tiles):
            out_ref[pl.ds(tile * 8, 8), lanes] = sums[tile]


def lane_scatter(values, index):
    count = values.shape[0]
    padded = -(-count // BLOCK) * BLOCK
    values_t = jnp.pad(values, ((0, padded - count), (0, 0))).T
    index_t = jnp.pad(index, ((0, padded - count), (0, 0))).T
    out = pl.pallas_call(
        lane_scatter_kernel,
        out_shape=jax.ShapeDtypeStruct((BLOCK, padded), values.dtype),
    )(values_t, index_t)
    return out.T[:count]


def gather_blocks(table, blocks, rows):
    lead = table.shape[:-1]
    tiled = table.reshape(lead + (-1, BLOCK))
    picked = jnp.take(tiled, blocks, axis=-2)
    index = jnp.broadcast_to(rows.reshape(-1, BLOCK), picked.shape)
    values = lane_gather(picked.reshape(-1, BLOCK), index.reshape(-1, BLOCK))
    return values.reshape(lead + (-1,))


def scatter_blocks(values, blocks, rows, count):
    lead = values.shape[:-1]
    tiled = values.reshape(lead + (-1, BLOCK))
    index = jnp.broadcast_to(rows.reshape(-1, BLOCK), tiled.shape)
    within = lane_scatter(tiled.reshape(-1, BLOCK), index.reshape(-1, BLOCK))
    within = within.reshape(tiled.shape)
    out = jnp.zeros(lead + (count, BLOCK), values.dtype)
    out = out.at[..., blocks, :].add(within)
    return out.reshape(lead + (-1,))


def chain_with_fillers(value, axis, fillers):
    count = lax.axis_size(axis)
    state = None
    for index, mask in enumerate(butterfly_masks(count)):
        pairs = [(source, source ^ mask) for source in range(count)]
        if index in fillers:
            value, state = lax.optimization_barrier((value, state))
            state = fillers[index](state)
        value = value + lax.ppermute(value, axis, pairs)
        if index in fillers:
            value, state = lax.optimization_barrier((value, state))
    return value, state


def body(
    direction_nodal,
    direction_capacity,
    residual_nodal,
    residual_capacity,
    scale_flow,
    scale_dispatch,
    scale_storage,
    scale_capacity,
    availability,
    retention,
    line_anchor,
    line_target,
    anchor_rows,
    target_rows,
    column_block,
    column_rows,
):
    net_count = lax.axis_size("net")
    net_index = lax.axis_index("net")
    lines = anchor_rows.shape[0]

    partial_sums = -jnp.sum(availability[None] * direction_capacity, axis=1)

    balance = direction_nodal[:, :, 0, :]
    storage = direction_nodal[:, :, 1, :]
    buses = balance.shape[-1] * net_count
    if net_count == 2:
        other = lax.ppermute(balance, "net", [(0, 1), (1, 0)])
        network = jnp.where(
            net_index == 0,
            jnp.concatenate([balance, other], axis=-1),
            jnp.concatenate([other, balance], axis=-1),
        )
    else:
        network = lax.all_gather(balance, "net", axis=2, tiled=True)

    blocks = jnp.concatenate([line_anchor, line_target, column_block])
    rows = jnp.concatenate([anchor_rows, target_rows, column_rows])
    gathered = gather_blocks(network, blocks, rows)
    flow_value = gathered[..., :lines] - gathered[..., lines : 2 * lines]
    dispatch_value = gathered[..., 2 * lines :] + direction_capacity

    first_hour, gathered = lax.optimization_barrier((storage[:, :1], gathered))
    next_first = passed_along(first_hour, "tm", -1)
    storage_next = jnp.concatenate([storage[:, 1:, :], next_first], axis=1)
    level_value = storage - retention * storage_next
    charge_value = balance - storage
    flow_scaled = scale_flow[None] * flow_value
    dispatch_scaled = scale_dispatch[None] * dispatch_value
    level_scaled = scale_storage[None, :, 0, :] * level_value
    charge_scaled = scale_storage[None, :, 1, :] * charge_value
    nodal_rows = residual_nodal.reshape(residual_nodal.shape[0], -1, BLOCK)
    capacity_rows = residual_capacity.reshape(residual_capacity.shape[0], -1, BLOCK)
    squares_local = jnp.sum(nodal_rows * nodal_rows, axis=(1, 2)) + jnp.sum(
        capacity_rows * capacity_rows, axis=(1, 2)
    )

    curvature_local = (
        jnp.sum(flow_scaled * flow_value, axis=(1, 2))
        + jnp.sum(
            dispatch_scaled * dispatch_value + DAMPING * direction_capacity * direction_capacity,
            axis=(1, 2),
        )
        + jnp.sum(
            charge_scaled * charge_value
            + level_scaled * level_value
            + DAMPING * (balance * balance + storage * storage),
            axis=(1, 2),
        )
    )
    columns = partial_sums.shape[-1]
    scalars = jnp.stack([squares_local, curvature_local], axis=-1)
    packed = jnp.concatenate(
        [partial_sums, jnp.pad(scalars, ((0, 0), (0, BLOCK - 2)))], axis=-1
    )
    scatter_values = jnp.concatenate([flow_scaled, -flow_scaled, dispatch_scaled], axis=-1)
    lead = scatter_values.shape[:-1]
    tiled = scatter_values.reshape(lead + (-1, BLOCK))
    scatter_index = jnp.broadcast_to(rows.reshape(-1, BLOCK), tiled.shape)

    def within_blocks(state):
        return lane_scatter(tiled.reshape(-1, BLOCK), scatter_index.reshape(-1, BLOCK))

    def onto_buses(within):
        out = jnp.zeros(lead + (buses // BLOCK, BLOCK), tiled.dtype)
        return out.at[..., blocks, :].add(within.reshape(tiled.shape)).reshape(lead + (-1,))

    steps = lax.axis_size("tm").bit_length() - 1
    if tm_count_is_power(lax.axis_size("tm")) and steps >= 3:
        first = min(2, steps - 2)
        packed, bus_terms = chain_with_fillers(
            packed, "tm", {first: within_blocks, first + 1: onto_buses}
        )
    else:
        packed = butterfly_sum(packed, "tm")
        bus_terms = onto_buses(within_blocks(None))
    capacity_value = packed[:, :columns]
    capacity_scaled = scale_capacity[None] * capacity_value
    capacity_part = jnp.sum(capacity_scaled * capacity_value, axis=1)
    sums = packed[:, columns : columns + 2] + jnp.stack(
        [jnp.zeros_like(capacity_part), capacity_part], axis=-1
    )
    image_limit = (
        dispatch_scaled
        - availability[None] * capacity_scaled[:, None, :]
        + DAMPING * direction_capacity
    )
    sums, image_limit = lax.optimization_barrier((sums, image_limit))
    totals = butterfly_sum(sums, "net")

    if net_count == 2:
        half = buses // 2
        mine = lax.dynamic_slice_in_dim(bus_terms, net_index * half, half, axis=-1)
        theirs = lax.dynamic_slice_in_dim(bus_terms, (1 - net_index) * half, half, axis=-1)
        own_terms = mine + lax.ppermute(theirs, "net", [(0, 1), (1, 0)])
    else:
        own_terms = lax.psum_scatter(bus_terms, "net", scatter_dimension=2, tiled=True)
    image_balance = own_terms + charge_scaled + DAMPING * balance
    behind = passed_along(level_scaled[:, -1:], "tm", 1)
    level_before = jnp.concatenate([behind, level_scaled[:, :-1, :]], axis=1)
    image_storage = level_scaled - retention * level_before - charge_scaled + DAMPING * storage
    image_nodal = jnp.stack([image_balance, image_storage], axis=2)
    step_size = totals[:, 0] / totals[:, 1]
    updated_nodal = residual_nodal - step_size[:, None, None, None] * image_nodal
    updated_capacity = residual_capacity - step_size[:, None, None] * image_limit
    return (updated_nodal, updated_capacity)


def solution(mesh):
    in_specs = (
        P(None, "tm", None, "net"),
        P(None, "tm", "net"),
        P(None, "tm", None, "net"),
        P(None, "tm", "net"),
        P("tm", "net"),
        P("tm", "net"),
        P("tm", None, "net"),
        P("net"),
        P("tm", "net"),
        P("net"),
        P("net"),
        P("net"),
        P("net"),
        P("net"),
        P("net"),
        P("net"),
    )
    out_specs = (P(None, "tm", None, "net"), P(None, "tm", "net"))
    return jax.shard_map(body, mesh=mesh, in_specs=in_specs, out_specs=out_specs, check_vma=False)
```
